128 devices in a mesh: dom: 64 (over z, y, x), col: 2 (over core).
Axes of the slice: x: 4, y: 4, z: 4, core: 2. Of those that a mesh axis runs over, the one named last changes fastest.
Arguments:
- features: bfloat16 [196608, 1024], P('dom', 'col'), may hold values from -6 to 6
- block_type: int32 [1536], P('dom'), may hold values from 0 to 2
- rel_weight: bfloat16 [16, 1024, 1024], P(None, None, 'col'), may hold values from -0.1875 to 0.1875
- self_weight: bfloat16 [3, 1024, 1024], P(None, None, 'col'), may hold values from -0.1875 to 0.1875
- source_relation: int32 [64, 64, 2], P('dom'), may hold values from 0 to 15
- source_block: int32 [64, 64, 2], P('dom'), may hold values from 0 to 23
- target_relation: int32 [64, 64, 2], P('dom'), may hold values from 0 to 15, as said below
- target_block: int32 [64, 64, 2], P('dom'), may hold values from 0 to 23
- live: int32 [64, 64, 2], P('dom'), may hold values from 0 to 1, as said below
- tiles: int32 [64, 64, 2, 128, 128], P('dom'), may hold values 0 or 1
Outputs:
- updated: bfloat16 [196608, 1024], P('dom', 'col')
The draws below stay inside these ranges and needn't reach their ends.
Inputs may be any that keep to these rules, and one draw needn't show every extreme that they name: For each destination q and source p, live[q, p, k] is 1 exactly for k below a count of 0 to 2; in every draw some destinations receive 2 live slots from every source. target_relation[q, p, k] equals source_relation[p, q, k].
All inputs are finite; a program needn't handle non-finite values. No bound on the sum of `tiles` on one device may be relied on, other than what follows from the above.
Results may differ from the reference program's by a relative error of at most 0.0034.
Values may be sent and summed in bfloat16 or wider, within the bound.
No kernel may reach another device: no remote copies, remote signals or barrier semaphores. Data moves between devices by JAX's collectives and lax.ppermute only.
A program may use at most 320 MiB of HBM per device.

```python
import jax
import jax.numpy as jnp
from jax import lax

D = 1024
RELS = 16
TYPES = 3
BLOCK = 128
CAP = 2
BLK_DEV = 24
NBLK = 1536
NODES = 196608
N_DOM = 64


def relation_table(key):
    return jax.random.randint(jax.random.fold_in(key, 11), (N_DOM, N_DOM, CAP), 0, RELS).astype(jnp.int32)


def draw_source_relation(key, part):
    return relation_table(key)


def draw_target_relation(key, part):
    return jnp.transpose(relation_table(key), (1, 0, 2))


def draw_live(key, part):
    shuffle = jax.random.permutation(jax.random.fold_in(key, 3), N_DOM)
    hotset = shuffle < max(N_DOM // 4, 1)
    counts = jax.random.randint(jax.random.fold_in(key, 5), (N_DOM, N_DOM), 0, CAP)
    counts = jnp.where(hotset[:, None], CAP, counts)
    slot_ids = jnp.arange(CAP)
    return (slot_ids[None, None, :] < counts[:, :, None]).astype(jnp.int32)


def set_ends(array, stream_key, smallest, largest):
    longest = array.shape.index(max(array.shape))
    spots = []
    for shift in (0, 1):
        where = [jax.random.randint(jax.random.fold_in(stream_key, axis), (), 0, length) for axis, length in enumerate(array.shape)]
        where[longest] = (where[longest] + shift) % array.shape[longest]
        spots.append(tuple(where))
    return array.at[spots[0]].set(smallest).at[spots[1]].set(largest)


def levels(own_key, shape, split, smallest, high):
    gain = 1.0
    for axis_at, blocks in split:
        heights = jax.random.uniform(jax.random.fold_in(jax.random.fold_in(own_key, 6), axis_at), (blocks,), jnp.float32, smallest / len(split), high / len(split))
        gain = gain * jnp.repeat(jnp.exp(heights), shape[axis_at] // blocks).reshape((-1,) + (1,) * (len(shape) - 1 - axis_at))
    return gain


def gaussian(own_key, extent, spread, reach, cuts=(), kind=jnp.bfloat16):
    factor_of = levels(own_key, extent, cuts, -0.22, 0.18) if cuts else 1.0
    values = jax.random.normal(own_key, extent, jnp.float32) * spread * factor_of
    return jnp.minimum(jnp.maximum(values, -reach), reach).astype(kind)


def setup_inputs(seed: int = 0) -> dict:
    key_list = jax.random.split(jax.random.key(seed), 11)
    return {
        "features": gaussian(key_list[0], (NODES, D), 1.0, 6.0, ((0, 64), (1, 2))),
        "block_type": set_ends(jax.random.randint(key_list[1], (NBLK,), 0, TYPES), jax.random.fold_in(key_list[1], 1), 0, TYPES - 1).astype(jnp.int32),
        "rel_weight": gaussian(key_list[2], (RELS, D, D), D ** -0.5, 0.1875, ((2, 2),)),
        "self_weight": gaussian(key_list[3], (TYPES, D, D), D ** -0.5, 0.1875, ((2, 2),)),
        "source_relation": draw_source_relation(jax.random.fold_in(key_list[10], 71), 0),
        "source_block": set_ends(jax.random.randint(key_list[5], (N_DOM, N_DOM, CAP), 0, BLK_DEV), jax.random.fold_in(key_list[5], 1), 0, BLK_DEV - 1).astype(jnp.int32),
        "target_relation": draw_target_relation(jax.random.fold_in(key_list[10], 71), 0),
        "target_block": set_ends(jax.random.randint(key_list[7], (N_DOM, N_DOM, CAP), 0, BLK_DEV), jax.random.fold_in(key_list[7], 1), 0, BLK_DEV - 1).astype(jnp.int32),
        "live": draw_live(jax.random.fold_in(key_list[10], 71), 0),
        "tiles": set_ends((jax.random.randint(key_list[9], (N_DOM, N_DOM, CAP, BLOCK, BLOCK), 0, 16) < 1).astype(jnp.int32), jax.random.fold_in(key_list[9], 1), 0, 1),
    }


def reference(features, block_type, rel_weight, self_weight, source_relation, source_block, target_relation, target_block, live, tiles):
    blocks = features.reshape(N_DOM, BLK_DEV, BLOCK, D)
    types = block_type.reshape(N_DOM, BLK_DEV)
    key_range = jnp.arange(RELS * BLK_DEV).astype(jnp.int32)

    def one_target(index):
        adjacency = tiles[index].astype(jnp.float32) * live[index].astype(jnp.float32)[:, :, None, None]
        row_sums = jnp.sum(adjacency, axis=3)
        keys = (target_relation[index] * BLK_DEV + target_block[index]).astype(jnp.int32)
        table = (keys[:, :, None] == key_range[None, None, :]).astype(jnp.float32)
        degree = jnp.einsum('pkt,pki->ti', table, row_sums, precision=lax.Precision.HIGHEST)
        inverse = 1.0 / jnp.maximum(degree, 1.0)
        scale = jnp.einsum('pkt,ti->pki', table, inverse, precision=lax.Precision.HIGHEST)

        def one_slot(total, slot):
            source = (slot // CAP).astype(jnp.int32)
            place = (slot % CAP).astype(jnp.int32)
            rows = blocks[source, source_block[source, index, place]]
            message = jnp.dot(rows, rel_weight[source_relation[source, index, place]], preferred_element_type=jnp.float32).astype(jnp.bfloat16)
            summed = jnp.dot(adjacency[source, place], message.astype(jnp.float32), precision=lax.Precision.HIGHEST)
            term = scale[source, place][:, None] * summed
            return total.at[target_block[index, source, place]].add(term), None

        start = jnp.zeros((BLK_DEV, BLOCK, D), jnp.float32)
        total, unused = lax.scan(one_slot, start, jnp.arange(N_DOM * CAP).astype(jnp.int32))

        def self_one(pair):
            return jnp.dot(pair[0], self_weight[pair[1]], preferred_element_type=jnp.float32)

        selfs = lax.map(self_one, (blocks[index], types[index]))
        return (total + selfs).astype(jnp.bfloat16)

    result = lax.map(one_target, jnp.arange(N_DOM).astype(jnp.int32))
    return result.reshape(N_DOM * BLK_DEV * BLOCK, D)
```

```python
import functools

import jax
import jax.numpy as jnp
from jax import lax
from jax.experimental import pallas as pl
from jax.experimental.pallas import tpu as pltpu
from jax.sharding import PartitionSpec as P


def _bmm_kernel(dst_ref, src_ref, widx_ref, x_ref, w_ref, o_ref):
    o_ref[...] = jnp.dot(x_ref[...], w_ref[...], preferred_element_type=jnp.float32).astype(
        o_ref.dtype
    )


def _block_matmul(x, w, dst, src, widx, n_out, block_rows, out_dtype):
    k_dim = x.shape[1]
    n_dim = w.shape[2]
    steps = dst.shape[0]
    grid_spec = pltpu.PrefetchScalarGridSpec(
        num_scalar_prefetch=3,
        grid=(steps,),
        in_specs=[
            pl.BlockSpec((block_rows, k_dim), lambda s, d, r, g: (r[s], 0)),
            pl.BlockSpec((None, k_dim, n_dim), lambda s, d, r, g: (g[s], 0, 0)),
        ],
        out_specs=pl.BlockSpec((None, block_rows, n_dim), lambda s, d, r, g: (d[s], 0, 0)),
    )
    out_bytes = jnp.dtype(out_dtype).itemsize
    cost = pl.CostEstimate(
        flops=2 * steps * block_rows * k_dim * n_dim,
        bytes_accessed=steps * block_rows * (k_dim * 2 + n_dim * out_bytes) + w.size * 2,
        transcendentals=0,
    )
    return pl.pallas_call(
        _bmm_kernel,
        grid_spec=grid_spec,
        out_shape=jax.ShapeDtypeStruct((n_out, block_rows, n_dim), out_dtype),
        compiler_params=pltpu.CompilerParams(dimension_semantics=("arbitrary",)),
        cost_estimate=cost,
    )(dst, src, widx, x, w)


def _agg_kernel(tb_ref, live_ref, tiles_ref, msg_ref, inv_ref, acc_in_ref, acc_ref):
    s = pl.program_id(0)

    @pl.when(s == 0)
    def _():
        acc_ref[...] = acc_in_ref[...]

    block_rows = msg_ref.shape[0]
    adj = (tiles_ref[...] * live_ref[s]).astype(jnp.float32).astype(jnp.bfloat16)
    term = jnp.dot(adj, msg_ref[...], preferred_element_type=jnp.float32) * inv_ref[...]
    rows = pl.ds(pl.multiple_of(tb_ref[s] * block_rows, block_rows), block_rows)
    acc_ref[rows, :] += term


def _aggregate(acc, tiles, msgs, inv, tb, live, k):
    steps, block_rows, n_dim = msgs.shape
    rows = acc.shape[0]
    grid_spec = pltpu.PrefetchScalarGridSpec(
        num_scalar_prefetch=2,
        grid=(steps,),
        in_specs=[
            pl.BlockSpec((None, None, block_rows, block_rows), lambda s, t, l: (s, k, 0, 0)),
            pl.BlockSpec((None, block_rows, n_dim), lambda s, t, l: (s, 0, 0)),
            pl.BlockSpec((None, block_rows, 1), lambda s, t, l: (s, 0, 0)),
            pl.BlockSpec((rows, n_dim), lambda s, t, l: (0, 0)),
        ],
        out_specs=pl.BlockSpec((rows, n_dim), lambda s, t, l: (0, 0)),
    )
    cost = pl.CostEstimate(
        flops=2 * steps * block_rows * block_rows * n_dim,
        bytes_accessed=steps * block_rows * (block_rows * 4 + n_dim * 2 + 4) + 2 * rows * n_dim * 4,
        transcendentals=0,
    )
    return pl.pallas_call(
        _agg_kernel,
        grid_spec=grid_spec,
        out_shape=jax.ShapeDtypeStruct(acc.shape, jnp.float32),
        input_output_aliases={5: 0},
        compiler_params=pltpu.CompilerParams(
            dimension_semantics=("arbitrary",), vmem_limit_bytes=56 * 1024 * 1024
        ),
        cost_estimate=cost,
    )(tb, live, tiles, msgs, inv, acc)


def on_device(
    features,
    block_type,
    rel_weight,
    self_weight,
    source_relation,
    source_block,
    target_relation,
    target_block,
    live,
    tiles,
):
    blk_count = block_type.shape[0]
    rows_total = features.shape[0]
    block_rows = rows_total // blk_count
    relations = rel_weight.shape[0]
    partitions = live.shape[1]
    capacity = live.shape[2]
    slots = partitions * capacity

    full_rows = lax.all_gather(features, "col", axis=1, tiled=True)

    tiles4 = tiles.reshape(partitions, capacity, block_rows, block_rows)
    live2 = live.reshape(partitions, capacity)
    row_sums = (jnp.sum(tiles4, axis=3) * live2[:, :, None]).astype(jnp.float32)
    keys = target_relation.reshape(slots) * blk_count + target_block.reshape(slots)
    table = (keys[:, None] == jnp.arange(relations * blk_count)[None, :]).astype(jnp.float32)
    degree = jnp.dot(
        table.T, row_sums.reshape(slots, block_rows), precision=lax.Precision.HIGHEST
    )
    inverse = 1.0 / jnp.maximum(degree, 1.0)
    scale = jnp.dot(table, inverse, precision=lax.Precision.HIGHEST)
    scale = scale.reshape(partitions, capacity, block_rows, 1)

    src_blocks = source_block.reshape(partitions, capacity)
    src_rels = source_relation.reshape(partitions, capacity)
    dst_blocks = target_block.reshape(partitions, capacity)

    arrived = []
    for k in range(capacity):
        rel_k = src_rels[:, k]
        order = jnp.argsort(rel_k).astype(jnp.int32)
        msgs = _block_matmul(
            full_rows,
            rel_weight,
            order,
            src_blocks[:, k][order],
            rel_k[order],
            partitions,
            block_rows,
            jnp.bfloat16,
        )
        arrived.append(lax.all_to_all(msgs, "dom", split_axis=0, concat_axis=0, tiled=True))

    type_order = jnp.argsort(block_type).astype(jnp.int32)
    selfs = _block_matmul(
        full_rows,
        self_weight,
        type_order,
        type_order,
        block_type[type_order],
        blk_count,
        block_rows,
        jnp.float32,
    )
    acc = selfs.reshape(rows_total, selfs.shape[2])
    for k in range(capacity):
        acc = _aggregate(
            acc, tiles4, arrived[k], scale[:, k], dst_blocks[:, k], live2[:, k], k
        )
    return acc.astype(jnp.bfloat16)


def solution(mesh):
    in_specs = (
        P("dom", "col"),
        P("dom"),
        P(None, None, "col"),
        P(None, None, "col"),
        P("dom", None, None),
        P("dom", None, None),
        P("dom", None, None),
        P("dom", None, None),
        P("dom", None, None),
        P("dom", None, None, None, None),
    )
    out_specs = P("dom", "col")
    return jax.shard_map(
        on_device, mesh=mesh, in_specs=in_specs, out_specs=out_specs, check_vma=False
    )
```

```python
import functools

import jax
import jax.numpy as jnp
from jax import lax
from jax.experimental import pallas as pl
from jax.experimental.pallas import tpu as pltpu
from jax.sharding import PartitionSpec as P


def _bmm_kernel(group, src_ref, widx_ref, x_ref, w_ref, o_ref):
    step = pl.program_id(0)
    block_rows = o_ref.shape[1]
    for j in range(group):
        slot = step * group + j
        rows = pl.ds(pl.multiple_of(src_ref[slot] * block_rows, block_rows), block_rows)
        o_ref[j] = jnp.dot(
            x_ref[rows, :], w_ref[widx_ref[slot]], preferred_element_type=jnp.float32
        ).astype(o_ref.dtype)


def _block_matmul(x, w, src, widx, block_rows, out_dtype, group=8):
    k_dim = x.shape[1]
    n_dim = w.shape[2]
    steps = src.shape[0]
    grid_spec = pltpu.PrefetchScalarGridSpec(
        num_scalar_prefetch=2,
        grid=(steps // group,),
        in_specs=[
            pl.BlockSpec(x.shape, lambda i, r, g: (0, 0), pipeline_mode=pl.Buffered(1)),
            pl.BlockSpec(w.shape, lambda i, r, g: (0, 0, 0), pipeline_mode=pl.Buffered(1)),
        ],
        out_specs=pl.BlockSpec((group, block_rows, n_dim), lambda i, r, g: (i, 0, 0)),
    )
    out_bytes = jnp.dtype(out_dtype).itemsize
    cost = pl.CostEstimate(
        flops=2 * steps * block_rows * k_dim * n_dim,
        bytes_accessed=x.size * 2 + w.size * 2 + steps * block_rows * n_dim * out_bytes,
        transcendentals=0,
    )
    return pl.pallas_call(
        functools.partial(_bmm_kernel, group),
        grid_spec=grid_spec,
        out_shape=jax.ShapeDtypeStruct((steps, block_rows, n_dim), out_dtype),
        compiler_params=pltpu.CompilerParams(
            dimension_semantics=("arbitrary",), vmem_limit_bytes=48 * 1024 * 1024
        ),
        cost_estimate=cost,
    )(src, widx, x, w)


def _agg_kernel(group, final, tb_ref, live_ref, tiles_ref, msg_ref, inv_ref, acc_in_ref, out_ref, *scratch):
    step = pl.program_id(0)
    acc_ref = scratch[0] if final else out_ref

    @pl.when(step == 0)
    def _():
        acc_ref[...] = acc_in_ref[...]

    block_rows = msg_ref.shape[1]
    for j in range(group):
        slot = step * group + j
        adj = (tiles_ref[j] * live_ref[slot]).astype(jnp.float32).astype(jnp.bfloat16)
        term = jnp.dot(adj, msg_ref[j], preferred_element_type=jnp.float32) * inv_ref[j]
        rows = pl.ds(pl.multiple_of(tb_ref[slot] * block_rows, block_rows), block_rows)
        acc_ref[rows, :] += term

    if final:
        @pl.when(step == pl.num_programs(0) - 1)
        def _():
            out_ref[...] = acc_ref[...].astype(out_ref.dtype)


def _aggregate(acc, tiles, msgs, inv, tb, live, k, final, group=8):
    steps, block_rows, n_dim = msgs.shape
    rows = acc.shape[0]
    out_dtype = jnp.bfloat16 if final else jnp.float32
    grid_spec = pltpu.PrefetchScalarGridSpec(
        num_scalar_prefetch=2,
        grid=(steps // group,),
        in_specs=[
            pl.BlockSpec((group, None, block_rows, block_rows), lambda i, t, l: (i, k, 0, 0)),
            pl.BlockSpec((group, block_rows, n_dim), lambda i, t, l: (i, 0, 0)),
            pl.BlockSpec((group, block_rows, 1), lambda i, t, l: (i, 0, 0)),
            pl.BlockSpec((rows, n_dim), lambda i, t, l: (0, 0), pipeline_mode=pl.Buffered(1)),
        ],
        out_specs=pl.BlockSpec((rows, n_dim), lambda i, t, l: (0, 0)),
        scratch_shapes=[pltpu.VMEM((rows, n_dim), jnp.float32)] if final else [],
    )
    cost = pl.CostEstimate(
        flops=2 * steps * block_rows * block_rows * n_dim,
        bytes_accessed=steps * block_rows * (block_rows * 4 + n_dim * 2 + 4)
        + rows * n_dim * (4 + jnp.dtype(out_dtype).itemsize),
        transcendentals=0,
    )
    return pl.pallas_call(
        functools.partial(_agg_kernel, group, final),
        grid_spec=grid_spec,
        out_shape=jax.ShapeDtypeStruct(acc.shape, out_dtype),
        compiler_params=pltpu.CompilerParams(
            dimension_semantics=("arbitrary",), vmem_limit_bytes=56 * 1024 * 1024
        ),
        cost_estimate=cost,
    )(tb, live, tiles, msgs, inv, acc)


def on_device(
    features,
    block_type,
    rel_weight,
    self_weight,
    source_relation,
    source_block,
    target_relation,
    target_block,
    live,
    tiles,
):
    blk_count = block_type.shape[0]
    rows_total = features.shape[0]
    block_rows = rows_total // blk_count
    relations = rel_weight.shape[0]
    partitions = live.shape[1]
    capacity = live.shape[2]
    slots = partitions * capacity

    full_rows = lax.all_gather(features, "col", axis=1, tiled=True)

    tiles4 = tiles.reshape(partitions, capacity, block_rows, block_rows)
    live2 = live.reshape(partitions, capacity)
    row_sums = (jnp.sum(tiles4, axis=3) * live2[:, :, None]).astype(jnp.float32)
    keys = target_relation.reshape(slots) * blk_count + target_block.reshape(slots)
    table = (keys[:, None] == jnp.arange(relations * blk_count)[None, :]).astype(jnp.float32)
    degree = jnp.dot(
        table.T, row_sums.reshape(slots, block_rows), precision=lax.Precision.HIGHEST
    )
    inverse = 1.0 / jnp.maximum(degree, 1.0)
    scale = jnp.dot(table, inverse, precision=lax.Precision.HIGHEST)
    scale = scale.reshape(partitions, capacity, block_rows, 1)

    src_blocks = source_block.reshape(partitions, capacity)
    src_rels = source_relation.reshape(partitions, capacity)
    dst_blocks = target_block.reshape(partitions, capacity)

    arrived = []
    for k in range(capacity):
        msgs = _block_matmul(
            full_rows, rel_weight, src_blocks[:, k], src_rels[:, k], block_rows, jnp.bfloat16
        )
        arrived.append(lax.all_to_all(msgs, "dom", split_axis=0, concat_axis=0, tiled=True))

    selfs = _block_matmul(
        full_rows,
        self_weight,
        jnp.arange(blk_count, dtype=jnp.int32),
        block_type,
        block_rows,
        jnp.float32,
    )
    acc = selfs.reshape(rows_total, selfs.shape[2])
    for k in range(capacity):
        acc = _aggregate(
            acc,
            tiles4,
            arrived[k],
            scale[:, k],
            dst_blocks[:, k],
            live2[:, k],
            k,
            final=k == capacity - 1,
        )
    return acc


def solution(mesh):
    in_specs = (
        P("dom", "col"),
        P("dom"),
        P(None, None, "col"),
        P(None, None, "col"),
        P("dom", None, None),
        P("dom", None, None),
        P("dom", None, None),
        P("dom", None, None),
        P("dom", None, None),
        P("dom", None, None, None, None),
    )
    out_specs = P("dom", "col")
    return jax.shard_map(
        on_device, mesh=mesh, in_specs=in_specs, out_specs=out_specs, check_vma=False
    )
```

```python
import functools

import jax
import jax.numpy as jnp
from jax import lax
from jax.experimental import pallas as pl
from jax.experimental.pallas import tpu as pltpu
from jax.sharding import PartitionSpec as P


def _bmm_kernel(group, src_ref, widx_ref, x_ref, w_ref, o_ref):
    step = pl.program_id(0)
    block_rows = o_ref.shape[1]
    for j in range(group):
        slot = step * group + j
        rows = pl.ds(pl.multiple_of(src_ref[slot] * block_rows, block_rows), block_rows)
        o_ref[j] = jnp.dot(
            x_ref[rows, :], w_ref[widx_ref[slot]], preferred_element_type=jnp.float32
        ).astype(o_ref.dtype)


def _block_matmul(x, w, src, widx, block_rows, out_dtype, group=8):
    k_dim = x.shape[1]
    n_dim = w.shape[2]
    steps = src.shape[0]
    grid_spec = pltpu.PrefetchScalarGridSpec(
        num_scalar_prefetch=2,
        grid=(steps // group,),
        in_specs=[
            pl.BlockSpec(x.shape, lambda i, r, g: (0, 0), pipeline_mode=pl.Buffered(1)),
            pl.BlockSpec(w.shape, lambda i, r, g: (0, 0, 0), pipeline_mode=pl.Buffered(1)),
        ],
        out_specs=pl.BlockSpec((group, block_rows, n_dim), lambda i, r, g: (i, 0, 0)),
    )
    out_bytes = jnp.dtype(out_dtype).itemsize
    cost = pl.CostEstimate(
        flops=2 * steps * block_rows * k_dim * n_dim,
        bytes_accessed=x.size * 2 + w.size * 2 + steps * block_rows * n_dim * out_bytes,
        transcendentals=0,
    )
    return pl.pallas_call(
        functools.partial(_bmm_kernel, group),
        grid_spec=grid_spec,
        out_shape=jax.ShapeDtypeStruct((steps, block_rows, n_dim), out_dtype),
        compiler_params=pltpu.CompilerParams(
            dimension_semantics=("arbitrary",), vmem_limit_bytes=56 * 1024 * 1024
        ),
        cost_estimate=cost,
    )(src, widx, x, w)


def _agg_kernel(group, final, tb_ref, live_ref, tiles_ref, msg_ref, inv_ref, acc_in_ref, out_ref, *scratch):
    step = pl.program_id(0)
    acc_ref = scratch[0] if final else out_ref

    @pl.when(step == 0)
    def _():
        acc_ref[...] = acc_in_ref[...]

    block_rows = msg_ref.shape[1]
    for j in range(group):
        slot = step * group + j
        adj = (tiles_ref[j] * live_ref[slot]).astype(jnp.float32).astype(jnp.bfloat16)
        term = jnp.dot(adj, msg_ref[j], preferred_element_type=jnp.float32) * inv_ref[j]
        rows = pl.ds(pl.multiple_of(tb_ref[slot] * block_rows, block_rows), block_rows)
        acc_ref[rows, :] += term

    if final:
        @pl.when(step == pl.num_programs(0) - 1)
        def _():
            out_ref[...] = acc_ref[...].astype(out_ref.dtype)


def _aggregate(acc, tiles, msgs, inv, tb, live, k, final, group=8):
    steps, block_rows, n_dim = msgs.shape
    rows = acc.shape[0]
    out_dtype = jnp.bfloat16 if final else jnp.float32
    grid_spec = pltpu.PrefetchScalarGridSpec(
        num_scalar_prefetch=2,
        grid=(steps // group,),
        in_specs=[
            pl.BlockSpec((group, None, block_rows, block_rows), lambda i, t, l: (i, k, 0, 0)),
            pl.BlockSpec((group, block_rows, n_dim), lambda i, t, l: (i, 0, 0)),
            pl.BlockSpec((group, block_rows, 1), lambda i, t, l: (i, 0, 0)),
            pl.BlockSpec((rows, n_dim), lambda i, t, l: (0, 0), pipeline_mode=pl.Buffered(1)),
        ],
        out_specs=pl.BlockSpec((rows, n_dim), lambda i, t, l: (0, 0)),
        scratch_shapes=[pltpu.VMEM((rows, n_dim), jnp.float32)] if final else [],
    )
    cost = pl.CostEstimate(
        flops=2 * steps * block_rows * block_rows * n_dim,
        bytes_accessed=steps * block_rows * (block_rows * 4 + n_dim * 2 + 4)
        + rows * n_dim * (4 + jnp.dtype(out_dtype).itemsize),
        transcendentals=0,
    )
    return pl.pallas_call(
        functools.partial(_agg_kernel, group, final),
        grid_spec=grid_spec,
        out_shape=jax.ShapeDtypeStruct(acc.shape, out_dtype),
        compiler_params=pltpu.CompilerParams(
            dimension_semantics=("arbitrary",), vmem_limit_bytes=56 * 1024 * 1024
        ),
        cost_estimate=cost,
    )(tb, live, tiles, msgs, inv, acc)


def on_device(
    features,
    block_type,
    rel_weight,
    self_weight,
    source_relation,
    source_block,
    target_relation,
    target_block,
    live,
    tiles,
):
    blk_count = block_type.shape[0]
    rows_total = features.shape[0]
    block_rows = rows_total // blk_count
    relations = rel_weight.shape[0]
    partitions = live.shape[1]
    capacity = live.shape[2]
    slots = partitions * capacity

    full_rows = lax.all_gather(features, "col", axis=1, tiled=True)

    tiles4 = tiles.reshape(partitions, capacity, block_rows, block_rows)
    live2 = live.reshape(partitions, capacity)
    row_sums = (jnp.sum(tiles4, axis=3) * live2[:, :, None]).astype(jnp.float32)
    keys = target_relation.reshape(slots) * blk_count + target_block.reshape(slots)
    table = (keys[:, None] == jnp.arange(relations * blk_count)[None, :]).astype(jnp.float32)
    degree = jnp.dot(
        table.T, row_sums.reshape(slots, block_rows), precision=lax.Precision.HIGHEST
    )
    inverse = 1.0 / jnp.maximum(degree, 1.0)
    scale = jnp.dot(table, inverse, precision=lax.Precision.HIGHEST)
    scale = scale.reshape(partitions, capacity, block_rows, 1)

    src_blocks = source_block.reshape(partitions, capacity)
    src_rels = source_relation.reshape(partitions, capacity)
    dst_blocks = target_block.reshape(partitions, capacity)

    feature_blocks = features.reshape(blk_count, block_rows, features.shape[1])
    raw = feature_blocks[src_blocks[:, 0]]
    arrived = [lax.all_to_all(raw, "dom", split_axis=0, concat_axis=0, tiled=True)]
    for k in range(1, capacity):
        msgs = _block_matmul(
            full_rows, rel_weight, src_blocks[:, k], src_rels[:, k], block_rows, jnp.bfloat16
        )
        arrived[0], msgs = lax.optimization_barrier((arrived[0], msgs))
        arrived.append(lax.all_to_all(msgs, "dom", split_axis=0, concat_axis=0, tiled=True))

    selfs = _block_matmul(
        full_rows,
        self_weight,
        jnp.arange(blk_count, dtype=jnp.int32),
        block_type,
        block_rows,
        jnp.float32,
    )
    acc = selfs.reshape(rows_total, selfs.shape[2])
    wide = lax.all_gather(arrived[0], "col", axis=2, tiled=True)
    arrived[0] = _block_matmul(
        wide.reshape(partitions * block_rows, wide.shape[2]),
        rel_weight,
        jnp.arange(partitions, dtype=jnp.int32),
        target_relation.reshape(partitions, capacity)[:, 0],
        block_rows,
        jnp.bfloat16,
    )
    for k in range(capacity):
        acc = _aggregate(
            acc,
            tiles4,
            arrived[k],
            scale[:, k],
            dst_blocks[:, k],
            live2[:, k],
            k,
            final=k == capacity - 1,
        )
    return acc


def solution(mesh):
    in_specs = (
        P("dom", "col"),
        P("dom"),
        P(None, None, "col"),
        P(None, None, "col"),
        P("dom", None, None),
        P("dom", None, None),
        P("dom", None, None),
        P("dom", None, None),
        P("dom", None, None),
        P("dom", None, None, None, None),
    )
    out_specs = P("dom", "col")
    return jax.shard_map(
        on_device, mesh=mesh, in_specs=in_specs, out_specs=out_specs, check_vma=False
    )
```

```python
import functools

import jax
import jax.numpy as jnp
from jax import lax
from jax.experimental import pallas as pl
from jax.experimental.pallas import tpu as pltpu
from jax.sharding import PartitionSpec as P


def _bmm_kernel(group, src_ref, widx_ref, x_ref, w_ref, o_ref):
    step = pl.program_id(0)
    block_rows = o_ref.shape[1]
    for j in range(group):
        slot = step * group + j
        rows = pl.ds(pl.multiple_of(src_ref[slot] * block_rows, block_rows), block_rows)
        o_ref[j] = jnp.dot(
            x_ref[rows, :], w_ref[widx_ref[slot]], preferred_element_type=jnp.float32
        ).astype(o_ref.dtype)


def _block_matmul(x, w, src, widx, block_rows, out_dtype, group=8):
    k_dim = x.shape[1]
    n_dim = w.shape[2]
    steps = src.shape[0]
    grid_spec = pltpu.PrefetchScalarGridSpec(
        num_scalar_prefetch=2,
        grid=(steps // group,),
        in_specs=[
            pl.BlockSpec(x.shape, lambda i, r, g: (0, 0), pipeline_mode=pl.Buffered(1)),
            pl.BlockSpec(w.shape, lambda i, r, g: (0, 0, 0), pipeline_mode=pl.Buffered(1)),
        ],
        out_specs=pl.BlockSpec((group, block_rows, n_dim), lambda i, r, g: (i, 0, 0)),
    )
    out_bytes = jnp.dtype(out_dtype).itemsize
    cost = pl.CostEstimate(
        flops=2 * steps * block_rows * k_dim * n_dim,
        bytes_accessed=x.size * 2 + w.size * 2 + steps * block_rows * n_dim * out_bytes,
        transcendentals=0,
    )
    return pl.pallas_call(
        functools.partial(_bmm_kernel, group),
        grid_spec=grid_spec,
        out_shape=jax.ShapeDtypeStruct((steps, block_rows, n_dim), out_dtype),
        compiler_params=pltpu.CompilerParams(
            dimension_semantics=("arbitrary",), vmem_limit_bytes=56 * 1024 * 1024
        ),
        cost_estimate=cost,
    )(src, widx, x, w)


def _agg_kernel(group, final, tb_ref, live_ref, tiles_ref, msg_ref, inv_ref, acc_in_ref, out_ref, *scratch):
    step = pl.program_id(0)
    acc_ref = scratch[0] if final else out_ref

    @pl.when(step == 0)
    def _():
        acc_ref[...] = acc_in_ref[...]

    block_rows = msg_ref.shape[1]
    for j in range(group):
        slot = step * group + j
        adj = (tiles_ref[j] * live_ref[slot]).astype(jnp.float32).astype(jnp.bfloat16)
        term = jnp.dot(adj, msg_ref[j], preferred_element_type=jnp.float32) * inv_ref[j]
        rows = pl.ds(pl.multiple_of(tb_ref[slot] * block_rows, block_rows), block_rows)
        acc_ref[rows, :] += term

    if final:
        @pl.when(step == pl.num_programs(0) - 1)
        def _():
            out_ref[...] = acc_ref[...].astype(out_ref.dtype)


def _aggregate(acc, tiles, msgs, inv, tb, live, k, final, group=8):
    steps, block_rows, n_dim = msgs.shape
    rows = acc.shape[0]
    out_dtype = jnp.bfloat16 if final else jnp.float32
    grid_spec = pltpu.PrefetchScalarGridSpec(
        num_scalar_prefetch=2,
        grid=(steps // group,),
        in_specs=[
            pl.BlockSpec((group, None, block_rows, block_rows), lambda i, t, l: (i, k, 0, 0)),
            pl.BlockSpec((group, block_rows, n_dim), lambda i, t, l: (i, 0, 0)),
            pl.BlockSpec((group, block_rows, 1), lambda i, t, l: (i, 0, 0)),
            pl.BlockSpec((rows, n_dim), lambda i, t, l: (0, 0), pipeline_mode=pl.Buffered(1)),
        ],
        out_specs=pl.BlockSpec((rows, n_dim), lambda i, t, l: (0, 0)),
        scratch_shapes=[pltpu.VMEM((rows, n_dim), jnp.float32)] if final else [],
    )
    cost = pl.CostEstimate(
        flops=2 * steps * block_rows * block_rows * n_dim,
        bytes_accessed=steps * block_rows * (block_rows * 4 + n_dim * 2 + 4)
        + rows * n_dim * (4 + jnp.dtype(out_dtype).itemsize),
        transcendentals=0,
    )
    return pl.pallas_call(
        functools.partial(_agg_kernel, group, final),
        grid_spec=grid_spec,
        out_shape=jax.ShapeDtypeStruct(acc.shape, out_dtype),
        compiler_params=pltpu.CompilerParams(
            dimension_semantics=("arbitrary",), vmem_limit_bytes=56 * 1024 * 1024
        ),
        cost_estimate=cost,
    )(tb, live, tiles, msgs, inv, acc)


def _widen(x, axis):
    other = lax.ppermute(x, "col", [(0, 1), (1, 0)])
    first = lax.axis_index("col") == 0
    low = jnp.where(first, x, other)
    high = jnp.where(first, other, x)
    return jnp.concatenate([low, high], axis=axis)


def on_device(
    features,
    block_type,
    rel_weight,
    self_weight,
    source_relation,
    source_block,
    target_relation,
    target_block,
    live,
    tiles,
):
    blk_count = block_type.shape[0]
    rows_total = features.shape[0]
    block_rows = rows_total // blk_count
    relations = rel_weight.shape[0]
    partitions = live.shape[1]
    capacity = live.shape[2]
    slots = partitions * capacity

    full_rows = _widen(features, 1)

    tiles4 = tiles.reshape(partitions, capacity, block_rows, block_rows)
    live2 = live.reshape(partitions, capacity)
    row_sums = (jnp.sum(tiles4, axis=3) * live2[:, :, None]).astype(jnp.float32)
    keys = target_relation.reshape(slots) * blk_count + target_block.reshape(slots)
    table = (keys[:, None] == jnp.arange(relations * blk_count)[None, :]).astype(jnp.float32)
    degree = jnp.dot(
        table.T, row_sums.reshape(slots, block_rows), precision=lax.Precision.HIGHEST
    )
    inverse = 1.0 / jnp.maximum(degree, 1.0)
    scale = jnp.dot(table, inverse, precision=lax.Precision.HIGHEST)
    scale = scale.reshape(partitions, capacity, block_rows, 1)

    src_blocks = source_block.reshape(partitions, capacity)
    src_rels = source_relation.reshape(partitions, capacity)
    dst_blocks = target_block.reshape(partitions, capacity)

    feature_blocks = features.reshape(blk_count, block_rows, features.shape[1])
    raw = feature_blocks[src_blocks[:, 0]]
    arrived = [lax.all_to_all(raw, "dom", split_axis=0, concat_axis=0, tiled=True)]
    for k in range(1, capacity):
        msgs = _block_matmul(
            full_rows, rel_weight, src_blocks[:, k], src_rels[:, k], block_rows, jnp.bfloat16
        )
        arrived[0], msgs = lax.optimization_barrier((arrived[0], msgs))
        arrived.append(lax.all_to_all(msgs, "dom", split_axis=0, concat_axis=0, tiled=True))

    selfs = _block_matmul(
        full_rows,
        self_weight,
        jnp.arange(blk_count, dtype=jnp.int32),
        block_type,
        block_rows,
        jnp.float32,
    )
    acc = selfs.reshape(rows_total, selfs.shape[2])
    wide = _widen(arrived[0], 2)
    arrived[0] = _block_matmul(
        wide.reshape(partitions * block_rows, wide.shape[2]),
        rel_weight,
        jnp.arange(partitions, dtype=jnp.int32),
        target_relation.reshape(partitions, capacity)[:, 0],
        block_rows,
        jnp.bfloat16,
    )
    for k in range(capacity):
        acc = _aggregate(
            acc,
            tiles4,
            arrived[k],
            scale[:, k],
            dst_blocks[:, k],
            live2[:, k],
            k,
            final=k == capacity - 1,
        )
    return acc


def solution(mesh):
    in_specs = (
        P("dom", "col"),
        P("dom"),
        P(None, None, "col"),
        P(None, None, "col"),
        P("dom", None, None),
        P("dom", None, None),
        P("dom", None, None),
        P("dom", None, None),
        P("dom", None, None),
        P("dom", None, None, None, None),
    )
    out_specs = P("dom", "col")
    return jax.shard_map(
        on_device, mesh=mesh, in_specs=in_specs, out_specs=out_specs, check_vma=False
    )
```

```python
import functools

import jax
import jax.numpy as jnp
from jax import lax
from jax.experimental import pallas as pl
from jax.experimental.pallas import tpu as pltpu
from jax.sharding import PartitionSpec as P


def _bmm_kernel(group, src_ref, widx_ref, x_ref, w_ref, o_ref):
    step = pl.program_id(0)
    block_rows = o_ref.shape[1]
    for j in range(group):
        slot = step * group + j
        rows = pl.ds(pl.multiple_of(src_ref[slot] * block_rows, block_rows), block_rows)
        o_ref[j] = jnp.dot(
            x_ref[rows, :], w_ref[widx_ref[slot]], preferred_element_type=jnp.float32
        ).astype(o_ref.dtype)


def _block_matmul(x, w, src, widx, block_rows, out_dtype, group=8):
    k_dim = x.shape[1]
    n_dim = w.shape[2]
    steps = src.shape[0]
    grid_spec = pltpu.PrefetchScalarGridSpec(
        num_scalar_prefetch=2,
        grid=(steps // group,),
        in_specs=[
            pl.BlockSpec(x.shape, lambda i, r, g: (0, 0), pipeline_mode=pl.Buffered(1)),
            pl.BlockSpec(w.shape, lambda i, r, g: (0, 0, 0), pipeline_mode=pl.Buffered(1)),
        ],
        out_specs=pl.BlockSpec((group, block_rows, n_dim), lambda i, r, g: (i, 0, 0)),
    )
    out_bytes = jnp.dtype(out_dtype).itemsize
    cost = pl.CostEstimate(
        flops=2 * steps * block_rows * k_dim * n_dim,
        bytes_accessed=x.size * 2 + w.size * 2 + steps * block_rows * n_dim * out_bytes,
        transcendentals=0,
    )
    return pl.pallas_call(
        functools.partial(_bmm_kernel, group),
        grid_spec=grid_spec,
        out_shape=jax.ShapeDtypeStruct((steps, block_rows, n_dim), out_dtype),
        compiler_params=pltpu.CompilerParams(
            dimension_semantics=("arbitrary",), vmem_limit_bytes=56 * 1024 * 1024
        ),
        cost_estimate=cost,
    )(src, widx, x, w)


def _pick_kernel(group, src_ref, x_ref, o_ref):
    step = pl.program_id(0)
    block_rows = o_ref.shape[1]
    for j in range(group):
        rows = pl.ds(pl.multiple_of(src_ref[step * group + j] * block_rows, block_rows), block_rows)
        o_ref[j] = x_ref[rows, :]


def _pick_blocks(x, src, block_rows, group=8):
    steps = src.shape[0]
    grid_spec = pltpu.PrefetchScalarGridSpec(
        num_scalar_prefetch=1,
        grid=(steps // group,),
        in_specs=[pl.BlockSpec(x.shape, lambda i, r: (0, 0), pipeline_mode=pl.Buffered(1))],
        out_specs=pl.BlockSpec((group, block_rows, x.shape[1]), lambda i, r: (i, 0, 0)),
    )
    return pl.pallas_call(
        functools.partial(_pick_kernel, group),
        grid_spec=grid_spec,
        out_shape=jax.ShapeDtypeStruct((steps, block_rows, x.shape[1]), x.dtype),
        compiler_params=pltpu.CompilerParams(dimension_semantics=("arbitrary",)),
        cost_estimate=pl.CostEstimate(
            flops=0, bytes_accessed=x.size * 2 + steps * block_rows * x.shape[1] * 2,
            transcendentals=0,
        ),
    )(src, x)


def _agg_kernel(group, final, tb_ref, live_ref, tiles_ref, msg_ref, inv_ref, acc_ref, out_ref):
    step = pl.program_id(0)
    block_rows = msg_ref.shape[1]
    for j in range(group):
        slot = step * group + j
        adj = (tiles_ref[j] * live_ref[slot]).astype(jnp.float32).astype(jnp.bfloat16)
        term = jnp.dot(adj, msg_ref[j], preferred_element_type=jnp.float32) * inv_ref[j]
        rows = pl.ds(pl.multiple_of(tb_ref[slot] * block_rows, block_rows), block_rows)
        acc_ref[rows, :] += term

    @pl.when(step == pl.num_programs(0) - 1)
    def _():
        out_ref[...] = acc_ref[...].astype(out_ref.dtype)


def _aggregate(acc, tiles, msgs, inv, tb, live, k, final, group=8):
    steps, block_rows, n_dim = msgs.shape
    rows = acc.shape[0]
    out_dtype = jnp.bfloat16 if final else jnp.float32
    grid_spec = pltpu.PrefetchScalarGridSpec(
        num_scalar_prefetch=2,
        grid=(steps // group,),
        in_specs=[
            pl.BlockSpec((group, None, block_rows, block_rows), lambda i, t, l: (i, k, 0, 0)),
            pl.BlockSpec((group, block_rows, n_dim), lambda i, t, l: (i, 0, 0)),
            pl.BlockSpec((group, block_rows, 1), lambda i, t, l: (i, 0, 0)),
            pl.BlockSpec((rows, n_dim), lambda i, t, l: (0, 0), pipeline_mode=pl.Buffered(1)),
        ],
        out_specs=pl.BlockSpec((rows, n_dim), lambda i, t, l: (0, 0)),
    )
    cost = pl.CostEstimate(
        flops=2 * steps * block_rows * block_rows * n_dim,
        bytes_accessed=steps * block_rows * (block_rows * 4 + n_dim * 2 + 4)
        + rows * n_dim * (4 + jnp.dtype(out_dtype).itemsize),
        transcendentals=0,
    )
    return pl.pallas_call(
        functools.partial(_agg_kernel, group, final),
        grid_spec=grid_spec,
        out_shape=jax.ShapeDtypeStruct(acc.shape, out_dtype),
        compiler_params=pltpu.CompilerParams(
            dimension_semantics=("arbitrary",), vmem_limit_bytes=56 * 1024 * 1024
        ),
        cost_estimate=cost,
    )(tb, live, tiles, msgs, inv, acc)


def _widen(x, axis):
    other = lax.ppermute(x, "col", [(0, 1), (1, 0)])
    first = lax.axis_index("col") == 0
    low = jnp.where(first, x, other)
    high = jnp.where(first, other, x)
    return jnp.concatenate([low, high], axis=axis)


def on_device(
    features,
    block_type,
    rel_weight,
    self_weight,
    source_relation,
    source_block,
    target_relation,
    target_block,
    live,
    tiles,
):
    blk_count = block_type.shape[0]
    rows_total = features.shape[0]
    block_rows = rows_total // blk_count
    relations = rel_weight.shape[0]
    partitions = live.shape[1]
    capacity = live.shape[2]
    slots = partitions * capacity

    full_rows = _widen(features, 1)

    tiles4 = tiles.reshape(partitions, capacity, block_rows, block_rows)
    live2 = live.reshape(partitions, capacity)
    row_sums = (jnp.sum(tiles4, axis=3) * live2[:, :, None]).astype(jnp.float32)
    keys = target_relation.reshape(slots) * blk_count + target_block.reshape(slots)
    table = (keys[:, None] == jnp.arange(relations * blk_count)[None, :]).astype(jnp.float32)
    degree = jnp.dot(
        table.T, row_sums.reshape(slots, block_rows), precision=lax.Precision.HIGHEST
    )
    inverse = 1.0 / jnp.maximum(degree, 1.0)
    scale = jnp.dot(table, inverse, precision=lax.Precision.HIGHEST)
    scale = scale.reshape(partitions, capacity, block_rows, 1)

    src_blocks = source_block.reshape(partitions, capacity)
    src_rels = source_relation.reshape(partitions, capacity)
    dst_blocks = target_block.reshape(partitions, capacity)

    raw = _pick_blocks(features, src_blocks[:, 0], block_rows)
    arrived = [lax.all_to_all(raw, "dom", split_axis=0, concat_axis=0, tiled=True)]
    for k in range(1, capacity):
        msgs = _block_matmul(
            full_rows, rel_weight, src_blocks[:, k], src_rels[:, k], block_rows, jnp.bfloat16
        )
        arrived[0], msgs = lax.optimization_barrier((arrived[0], msgs))
        arrived.append(lax.all_to_all(msgs, "dom", split_axis=0, concat_axis=0, tiled=True))

    selfs = _block_matmul(
        full_rows,
        self_weight,
        jnp.arange(blk_count, dtype=jnp.int32),
        block_type,
        block_rows,
        jnp.float32,
    )
    acc = selfs.reshape(rows_total, selfs.shape[2])
    wide = _widen(arrived[0], 2)
    arrived[0] = _block_matmul(
        wide.reshape(partitions * block_rows, wide.shape[2]),
        rel_weight,
        jnp.arange(partitions, dtype=jnp.int32),
        target_relation.reshape(partitions, capacity)[:, 0],
        block_rows,
        jnp.bfloat16,
    )
    for k in range(capacity):
        acc = _aggregate(
            acc,
            tiles4,
            arrived[k],
            scale[:, k],
            dst_blocks[:, k],
            live2[:, k],
            k,
            final=k == capacity - 1,
        )
    return acc


def solution(mesh):
    in_specs = (
        P("dom", "col"),
        P("dom"),
        P(None, None, "col"),
        P(None, None, "col"),
        P("dom", None, None),
        P("dom", None, None),
        P("dom", None, None),
        P("dom", None, None),
        P("dom", None, None),
        P("dom", None, None, None, None),
    )
    out_specs = P("dom", "col")
    return jax.shard_map(
        on_device, mesh=mesh, in_specs=in_specs, out_specs=out_specs, check_vma=False
    )
```

```python
import functools

import jax
import jax.numpy as jnp
from jax import lax
from jax.experimental import pallas as pl
from jax.experimental.pallas import tpu as pltpu
from jax.sharding import PartitionSpec as P


def _bmm_kernel(group, src_ref, widx_ref, col_ref, mine_ref, other_ref, w_ref, o_ref):
    step = pl.program_id(0)
    block_rows = o_ref.shape[1]
    first = col_ref[0] == 0
    for j in range(group):
        slot = step * group + j
        rows = pl.ds(pl.multiple_of(src_ref[slot] * block_rows, block_rows), block_rows)
        mine = mine_ref[rows, :]
        other = other_ref[rows, :]
        x = jnp.concatenate(
            [jnp.where(first, mine, other), jnp.where(first, other, mine)], axis=1
        )
        o_ref[j] = jnp.dot(
            x, w_ref[widx_ref[slot]], preferred_element_type=jnp.float32
        ).astype(o_ref.dtype)


def _block_matmul(halves, w, src, widx, block_rows, out_dtype, group=8):
    mine, other = halves
    k_dim = 2 * mine.shape[1]
    n_dim = w.shape[2]
    steps = src.shape[0]
    col = lax.axis_index("col").astype(jnp.int32).reshape(1)
    grid_spec = pltpu.PrefetchScalarGridSpec(
        num_scalar_prefetch=3,
        grid=(steps // group,),
        in_specs=[
            pl.BlockSpec(mine.shape, lambda i, r, g, c: (0, 0), pipeline_mode=pl.Buffered(1)),
            pl.BlockSpec(other.shape, lambda i, r, g, c: (0, 0), pipeline_mode=pl.Buffered(1)),
            pl.BlockSpec(w.shape, lambda i, r, g, c: (0, 0, 0), pipeline_mode=pl.Buffered(1)),
        ],
        out_specs=pl.BlockSpec((group, block_rows, n_dim), lambda i, r, g, c: (i, 0, 0)),
    )
    out_bytes = jnp.dtype(out_dtype).itemsize
    cost = pl.CostEstimate(
        flops=2 * steps * block_rows * k_dim * n_dim,
        bytes_accessed=mine.size * 4 + w.size * 2 + steps * block_rows * n_dim * out_bytes,
        transcendentals=0,
    )
    return pl.pallas_call(
        functools.partial(_bmm_kernel, group),
        grid_spec=grid_spec,
        out_shape=jax.ShapeDtypeStruct((steps, block_rows, n_dim), out_dtype),
        compiler_params=pltpu.CompilerParams(
            dimension_semantics=("arbitrary",), vmem_limit_bytes=56 * 1024 * 1024
        ),
        cost_estimate=cost,
    )(src, widx, col, mine, other, w)


def _pick_kernel(group, src_ref, x_ref, o_ref):
    step = pl.program_id(0)
    block_rows = o_ref.shape[1]
    for j in range(group):
        rows = pl.ds(pl.multiple_of(src_ref[step * group + j] * block_rows, block_rows), block_rows)
        o_ref[j] = x_ref[rows, :]


def _pick_blocks(x, src, block_rows, group=8):
    steps = src.shape[0]
    grid_spec = pltpu.PrefetchScalarGridSpec(
        num_scalar_prefetch=1,
        grid=(steps // group,),
        in_specs=[pl.BlockSpec(x.shape, lambda i, r: (0, 0), pipeline_mode=pl.Buffered(1))],
        out_specs=pl.BlockSpec((group, block_rows, x.shape[1]), lambda i, r: (i, 0, 0)),
    )
    return pl.pallas_call(
        functools.partial(_pick_kernel, group),
        grid_spec=grid_spec,
        out_shape=jax.ShapeDtypeStruct((steps, block_rows, x.shape[1]), x.dtype),
        compiler_params=pltpu.CompilerParams(dimension_semantics=("arbitrary",)),
        cost_estimate=pl.CostEstimate(
            flops=0, bytes_accessed=x.size * 2 + steps * block_rows * x.shape[1] * 2,
            transcendentals=0,
        ),
    )(src, x)


def _agg_kernel(group, final, tb_ref, live_ref, tiles_ref, msg_ref, inv_ref, acc_ref, out_ref):
    step = pl.program_id(0)
    block_rows = msg_ref.shape[1]
    for j in range(group):
        slot = step * group + j
        adj = (tiles_ref[j] * live_ref[slot]).astype(jnp.float32).astype(jnp.bfloat16)
        term = jnp.dot(adj, msg_ref[j], preferred_element_type=jnp.float32) * inv_ref[j]
        rows = pl.ds(pl.multiple_of(tb_ref[slot] * block_rows, block_rows), block_rows)
        acc_ref[rows, :] += term

    @pl.when(step == pl.num_programs(0) - 1)
    def _():
        out_ref[...] = acc_ref[...].astype(out_ref.dtype)


def _aggregate(acc, tiles, msgs, inv, tb, live, k, final, group=8):
    steps, block_rows, n_dim = msgs.shape
    rows = acc.shape[0]
    out_dtype = jnp.bfloat16 if final else jnp.float32
    grid_spec = pltpu.PrefetchScalarGridSpec(
        num_scalar_prefetch=2,
        grid=(steps // group,),
        in_specs=[
            pl.BlockSpec((group, None, block_rows, block_rows), lambda i, t, l: (i, k, 0, 0)),
            pl.BlockSpec((group, block_rows, n_dim), lambda i, t, l: (i, 0, 0)),
            pl.BlockSpec((group, block_rows, 1), lambda i, t, l: (i, 0, 0)),
            pl.BlockSpec((rows, n_dim), lambda i, t, l: (0, 0), pipeline_mode=pl.Buffered(1)),
        ],
        out_specs=pl.BlockSpec((rows, n_dim), lambda i, t, l: (0, 0)),
    )
    cost = pl.CostEstimate(
        flops=2 * steps * block_rows * block_rows * n_dim,
        bytes_accessed=steps * block_rows * (block_rows * 4 + n_dim * 2 + 4)
        + rows * n_dim * (4 + jnp.dtype(out_dtype).itemsize),
        transcendentals=0,
    )
    return pl.pallas_call(
        functools.partial(_agg_kernel, group, final),
        grid_spec=grid_spec,
        out_shape=jax.ShapeDtypeStruct(acc.shape, out_dtype),
        compiler_params=pltpu.CompilerParams(
            dimension_semantics=("arbitrary",), vmem_limit_bytes=56 * 1024 * 1024
        ),
        cost_estimate=cost,
    )(tb, live, tiles, msgs, inv, acc)


def _with_partner(x):
    return x, lax.ppermute(x, "col", [(0, 1), (1, 0)])


def on_device(
    features,
    block_type,
    rel_weight,
    self_weight,
    source_relation,
    source_block,
    target_relation,
    target_block,
    live,
    tiles,
):
    blk_count = block_type.shape[0]
    rows_total = features.shape[0]
    block_rows = rows_total // blk_count
    relations = rel_weight.shape[0]
    partitions = live.shape[1]
    capacity = live.shape[2]
    slots = partitions * capacity

    full_rows = _with_partner(features)

    tiles4 = tiles.reshape(partitions, capacity, block_rows, block_rows)
    live2 = live.reshape(partitions, capacity)
    row_sums = (jnp.sum(tiles4, axis=3) * live2[:, :, None]).astype(jnp.float32)
    keys = target_relation.reshape(slots) * blk_count + target_block.reshape(slots)
    table = (keys[:, None] == jnp.arange(relations * blk_count)[None, :]).astype(jnp.float32)
    degree = jnp.dot(
        table.T, row_sums.reshape(slots, block_rows), precision=lax.Precision.HIGHEST
    )
    inverse = 1.0 / jnp.maximum(degree, 1.0)
    scale = jnp.dot(table, inverse, precision=lax.Precision.HIGHEST)
    scale = scale.reshape(partitions, capacity, block_rows, 1)

    src_blocks = source_block.reshape(partitions, capacity)
    src_rels = source_relation.reshape(partitions, capacity)
    dst_blocks = target_block.reshape(partitions, capacity)

    raw = _pick_blocks(features, src_blocks[:, 0], block_rows)
    arrived = [lax.all_to_all(raw, "dom", split_axis=0, concat_axis=0, tiled=True)]
    for k in range(1, capacity):
        msgs = _block_matmul(
            full_rows, rel_weight, src_blocks[:, k], src_rels[:, k], block_rows, jnp.bfloat16
        )
        arrived[0], msgs = lax.optimization_barrier((arrived[0], msgs))
        arrived.append(lax.all_to_all(msgs, "dom", split_axis=0, concat_axis=0, tiled=True))

    selfs = _block_matmul(
        full_rows,
        self_weight,
        jnp.arange(blk_count, dtype=jnp.int32),
        block_type,
        block_rows,
        jnp.float32,
    )
    acc = selfs.reshape(rows_total, selfs.shape[2])
    mine, other = _with_partner(arrived[0])
    arrived[0] = _block_matmul(
        (
            mine.reshape(partitions * block_rows, mine.shape[2]),
            other.reshape(partitions * block_rows, other.shape[2]),
        ),
        rel_weight,
        jnp.arange(partitions, dtype=jnp.int32),
        target_relation.reshape(partitions, capacity)[:, 0],
        block_rows,
        jnp.bfloat16,
    )
    for k in range(capacity):
        acc = _aggregate(
            acc,
            tiles4,
            arrived[k],
            scale[:, k],
            dst_blocks[:, k],
            live2[:, k],
            k,
            final=k == capacity - 1,
        )
    return acc


def solution(mesh):
    in_specs = (
        P("dom", "col"),
        P("dom"),
        P(None, None, "col"),
        P(None, None, "col"),
        P("dom", None, None),
        P("dom", None, None),
        P("dom", None, None),
        P("dom", None, None),
        P("dom", None, None),
        P("dom", None, None, None, None),
    )
    out_specs = P("dom", "col")
    return jax.shard_map(
        on_device, mesh=mesh, in_specs=in_specs, out_specs=out_specs, check_vma=False
    )
```

```python
import functools

import jax
import jax.numpy as jnp
from jax import lax
from jax.experimental import pallas as pl
from jax.experimental.pallas import tpu as pltpu
from jax.sharding import PartitionSpec as P


def _bmm_kernel(group, src_ref, widx_ref, col_ref, mine_ref, other_ref, w_ref, o_ref):
    step = pl.program_id(0)
    block_rows = o_ref.shape[1]
    first = col_ref[0] == 0
    for j in range(group):
        slot = step * group + j
        rows = pl.ds(pl.multiple_of(src_ref[slot] * block_rows, block_rows), block_rows)
        mine = mine_ref[rows, :]
        other = other_ref[rows, :]
        x = jnp.concatenate(
            [jnp.where(first, mine, other), jnp.where(first, other, mine)], axis=1
        )
        o_ref[j] = jnp.dot(
            x, w_ref[widx_ref[slot]], preferred_element_type=jnp.float32
        ).astype(o_ref.dtype)


def _block_matmul(halves, w, src, widx, block_rows, out_dtype, group=8):
    mine, other = halves
    k_dim = 2 * mine.shape[1]
    n_dim = w.shape[2]
    steps = src.shape[0]
    col = lax.axis_index("col").astype(jnp.int32).reshape(1)
    grid_spec = pltpu.PrefetchScalarGridSpec(
        num_scalar_prefetch=3,
        grid=(steps // group,),
        in_specs=[
            pl.BlockSpec(mine.shape, lambda i, r, g, c: (0, 0), pipeline_mode=pl.Buffered(1)),
            pl.BlockSpec(other.shape, lambda i, r, g, c: (0, 0), pipeline_mode=pl.Buffered(1)),
            pl.BlockSpec(w.shape, lambda i, r, g, c: (0, 0, 0), pipeline_mode=pl.Buffered(1)),
        ],
        out_specs=pl.BlockSpec((group, block_rows, n_dim), lambda i, r, g, c: (i, 0, 0)),
    )
    out_bytes = jnp.dtype(out_dtype).itemsize
    cost = pl.CostEstimate(
        flops=2 * steps * block_rows * k_dim * n_dim,
        bytes_accessed=mine.size * 4 + w.size * 2 + steps * block_rows * n_dim * out_bytes,
        transcendentals=0,
    )
    return pl.pallas_call(
        functools.partial(_bmm_kernel, group),
        grid_spec=grid_spec,
        out_shape=jax.ShapeDtypeStruct((steps, block_rows, n_dim), out_dtype),
        compiler_params=pltpu.CompilerParams(
            dimension_semantics=("arbitrary",), vmem_limit_bytes=56 * 1024 * 1024
        ),
        cost_estimate=cost,
    )(src, widx, col, mine, other, w)


def _pick_kernel(group, src_ref, x_ref, o_ref):
    step = pl.program_id(0)
    block_rows = o_ref.shape[1]
    for j in range(group):
        rows = pl.ds(pl.multiple_of(src_ref[step * group + j] * block_rows, block_rows), block_rows)
        o_ref[j] = x_ref[rows, :]


def _pick_blocks(x, src, block_rows, group=8):
    steps = src.shape[0]
    grid_spec = pltpu.PrefetchScalarGridSpec(
        num_scalar_prefetch=1,
        grid=(steps // group,),
        in_specs=[pl.BlockSpec(x.shape, lambda i, r: (0, 0), pipeline_mode=pl.Buffered(1))],
        out_specs=pl.BlockSpec((group, block_rows, x.shape[1]), lambda i, r: (i, 0, 0)),
    )
    return pl.pallas_call(
        functools.partial(_pick_kernel, group),
        grid_spec=grid_spec,
        out_shape=jax.ShapeDtypeStruct((steps, block_rows, x.shape[1]), x.dtype),
        compiler_params=pltpu.CompilerParams(dimension_semantics=("arbitrary",)),
        cost_estimate=pl.CostEstimate(
            flops=0, bytes_accessed=x.size * 2 + steps * block_rows * x.shape[1] * 2,
            transcendentals=0,
        ),
    )(src, x)


def _agg_kernel(group, final, tb_ref, adj_ref, msg_ref, inv_ref, acc_ref, out_ref):
    step = pl.program_id(0)
    block_rows = msg_ref.shape[1]
    for j in range(group):
        slot = step * group + j
        term = jnp.dot(adj_ref[j], msg_ref[j], preferred_element_type=jnp.float32) * inv_ref[j]
        rows = pl.ds(pl.multiple_of(tb_ref[slot] * block_rows, block_rows), block_rows)
        acc_ref[rows, :] += term

    @pl.when(step == pl.num_programs(0) - 1)
    def _():
        out_ref[...] = acc_ref[...].astype(out_ref.dtype)


def _aggregate(acc, adj, msgs, inv, tb, k, final, group=16):
    steps, block_rows, n_dim = msgs.shape
    rows = acc.shape[0]
    out_dtype = jnp.bfloat16 if final else jnp.float32
    grid_spec = pltpu.PrefetchScalarGridSpec(
        num_scalar_prefetch=1,
        grid=(steps // group,),
        in_specs=[
            pl.BlockSpec((group, None, block_rows, block_rows), lambda i, t: (i, k, 0, 0)),
            pl.BlockSpec((group, block_rows, n_dim), lambda i, t: (i, 0, 0)),
            pl.BlockSpec((group, block_rows, 1), lambda i, t: (i, 0, 0)),
            pl.BlockSpec((rows, n_dim), lambda i, t: (0, 0), pipeline_mode=pl.Buffered(1)),
        ],
        out_specs=pl.BlockSpec((rows, n_dim), lambda i, t: (0, 0)),
    )
    cost = pl.CostEstimate(
        flops=2 * steps * block_rows * block_rows * n_dim,
        bytes_accessed=steps * block_rows * (block_rows * 2 + n_dim * 2 + 4)
        + rows * n_dim * (4 + jnp.dtype(out_dtype).itemsize),
        transcendentals=0,
    )
    return pl.pallas_call(
        functools.partial(_agg_kernel, group, final),
        grid_spec=grid_spec,
        out_shape=jax.ShapeDtypeStruct(acc.shape, out_dtype),
        compiler_params=pltpu.CompilerParams(
            dimension_semantics=("arbitrary",), vmem_limit_bytes=56 * 1024 * 1024
        ),
        cost_estimate=cost,
    )(tb, adj, msgs, inv, acc)


def _with_partner(x):
    return x, lax.ppermute(x, "col", [(0, 1), (1, 0)])


def on_device(
    features,
    block_type,
    rel_weight,
    self_weight,
    source_relation,
    source_block,
    target_relation,
    target_block,
    live,
    tiles,
):
    blk_count = block_type.shape[0]
    rows_total = features.shape[0]
    block_rows = rows_total // blk_count
    relations = rel_weight.shape[0]
    partitions = live.shape[1]
    capacity = live.shape[2]
    slots = partitions * capacity

    full_rows = _with_partner(features)

    tiles4 = tiles.reshape(partitions, capacity, block_rows, block_rows)
    live2 = live.reshape(partitions, capacity)
    row_sums = (jnp.sum(tiles4, axis=3) * live2[:, :, None]).astype(jnp.float32)
    keys = target_relation.reshape(slots) * blk_count + target_block.reshape(slots)
    table = (keys[:, None] == jnp.arange(relations * blk_count)[None, :]).astype(jnp.float32)
    degree = jnp.dot(
        table.T, row_sums.reshape(slots, block_rows), precision=lax.Precision.HIGHEST
    )
    inverse = 1.0 / jnp.maximum(degree, 1.0)
    scale = jnp.dot(table, inverse, precision=lax.Precision.HIGHEST)
    scale = scale.reshape(partitions, capacity, block_rows, 1)

    src_blocks = source_block.reshape(partitions, capacity)
    src_rels = source_relation.reshape(partitions, capacity)
    dst_blocks = target_block.reshape(partitions, capacity)

    raw = _pick_blocks(features, src_blocks[:, 0], block_rows)
    arrived = [lax.all_to_all(raw, "dom", split_axis=0, concat_axis=0, tiled=True)]
    for k in range(1, capacity):
        msgs = _block_matmul(
            full_rows, rel_weight, src_blocks[:, k], src_rels[:, k], block_rows, jnp.bfloat16
        )
        arrived[0], msgs = lax.optimization_barrier((arrived[0], msgs))
        arrived.append(lax.all_to_all(msgs, "dom", split_axis=0, concat_axis=0, tiled=True))

    selfs = _block_matmul(
        full_rows,
        self_weight,
        jnp.arange(blk_count, dtype=jnp.int32),
        block_type,
        block_rows,
        jnp.float32,
    )
    acc = selfs.reshape(rows_total, selfs.shape[2])
    mine, other = _with_partner(arrived[0])
    arrived[0] = _block_matmul(
        (
            mine.reshape(partitions * block_rows, mine.shape[2]),
            other.reshape(partitions * block_rows, other.shape[2]),
        ),
        rel_weight,
        jnp.arange(partitions, dtype=jnp.int32),
        target_relation.reshape(partitions, capacity)[:, 0],
        block_rows,
        jnp.bfloat16,
    )
    adjacency = (tiles4 * live2[:, :, None, None]).astype(jnp.bfloat16)
    for k in range(capacity):
        acc = _aggregate(
            acc,
            adjacency,
            arrived[k],
            scale[:, k],
            dst_blocks[:, k],
            k,
            final=k == capacity - 1,
        )
    return acc


def solution(mesh):
    in_specs = (
        P("dom", "col"),
        P("dom"),
        P(None, None, "col"),
        P(None, None, "col"),
        P("dom", None, None),
        P("dom", None, None),
        P("dom", None, None),
        P("dom", None, None),
        P("dom", None, None),
        P("dom", None, None, None, None),
    )
    out_specs = P("dom", "col")
    return jax.shard_map(
        on_device, mesh=mesh, in_specs=in_specs, out_specs=out_specs, check_vma=False
    )
```

```python
import functools

import jax
import jax.numpy as jnp
from jax import lax
from jax.experimental import pallas as pl
from jax.experimental.pallas import tpu as pltpu
from jax.sharding import PartitionSpec as P


def _bmm_kernel(group, src_ref, widx_ref, col_ref, mine_ref, other_ref, w_ref, o_ref):
    step = pl.program_id(0)
    block_rows = o_ref.shape[1]
    first = col_ref[0] == 0
    for j in range(group):
        slot = step * group + j
        rows = pl.ds(pl.multiple_of(src_ref[slot] * block_rows, block_rows), block_rows)
        mine = mine_ref[rows, :]
        other = other_ref[rows, :]
        x = jnp.concatenate(
            [jnp.where(first, mine, other), jnp.where(first, other, mine)], axis=1
        )
        o_ref[j] = jnp.dot(
            x, w_ref[widx_ref[slot]], preferred_element_type=jnp.float32
        ).astype(o_ref.dtype)


def _block_matmul(halves, w, src, widx, block_rows, out_dtype, group=8):
    mine, other = halves
    k_dim = 2 * mine.shape[1]
    n_dim = w.shape[2]
    steps = src.shape[0]
    col = lax.axis_index("col").astype(jnp.int32).reshape(1)
    grid_spec = pltpu.PrefetchScalarGridSpec(
        num_scalar_prefetch=3,
        grid=(steps // group,),
        in_specs=[
            pl.BlockSpec(mine.shape, lambda i, r, g, c: (0, 0), pipeline_mode=pl.Buffered(1)),
            pl.BlockSpec(other.shape, lambda i, r, g, c: (0, 0), pipeline_mode=pl.Buffered(1)),
            pl.BlockSpec(w.shape, lambda i, r, g, c: (0, 0, 0), pipeline_mode=pl.Buffered(1)),
        ],
        out_specs=pl.BlockSpec((group, block_rows, n_dim), lambda i, r, g, c: (i, 0, 0)),
    )
    out_bytes = jnp.dtype(out_dtype).itemsize
    cost = pl.CostEstimate(
        flops=2 * steps * block_rows * k_dim * n_dim,
        bytes_accessed=mine.size * 4 + w.size * 2 + steps * block_rows * n_dim * out_bytes,
        transcendentals=0,
    )
    return pl.pallas_call(
        functools.partial(_bmm_kernel, group),
        grid_spec=grid_spec,
        out_shape=jax.ShapeDtypeStruct((steps, block_rows, n_dim), out_dtype),
        compiler_params=pltpu.CompilerParams(
            dimension_semantics=("arbitrary",), vmem_limit_bytes=56 * 1024 * 1024
        ),
        cost_estimate=cost,
    )(src, widx, col, mine, other, w)


def _pick_kernel(group, src_ref, x_hbm, o_ref, sems):
    step = pl.program_id(0)
    block_rows = o_ref.shape[1]
    copies = []
    for j in range(group):
        rows = pl.ds(pl.multiple_of(src_ref[step * group + j] * block_rows, block_rows), block_rows)
        copy = pltpu.make_async_copy(x_hbm.at[rows, :], o_ref.at[j], sems.at[j])
        copy.start()
        copies.append(copy)
    for copy in copies:
        copy.wait()


def _pick_blocks(x, src, block_rows, group=8):
    steps = src.shape[0]
    grid_spec = pltpu.PrefetchScalarGridSpec(
        num_scalar_prefetch=1,
        grid=(steps // group,),
        in_specs=[pl.BlockSpec(memory_space=pl.ANY)],
        out_specs=pl.BlockSpec((group, block_rows, x.shape[1]), lambda i, r: (i, 0, 0)),
        scratch_shapes=[pltpu.SemaphoreType.DMA((group,))],
    )
    return pl.pallas_call(
        functools.partial(_pick_kernel, group),
        grid_spec=grid_spec,
        out_shape=jax.ShapeDtypeStruct((steps, block_rows, x.shape[1]), x.dtype),
        compiler_params=pltpu.CompilerParams(dimension_semantics=("arbitrary",)),
        cost_estimate=pl.CostEstimate(
            flops=0, bytes_accessed=2 * steps * block_rows * x.shape[1] * 2, transcendentals=0
        ),
    )(src, x)


def _agg_kernel(group, final, tb_ref, adj_ref, msg_ref, inv_ref, acc_ref, out_ref):
    step = pl.program_id(0)
    block_rows = msg_ref.shape[1]
    for j in range(group):
        slot = step * group + j
        term = jnp.dot(adj_ref[j], msg_ref[j], preferred_element_type=jnp.float32) * inv_ref[j]
        rows = pl.ds(pl.multiple_of(tb_ref[slot] * block_rows, block_rows), block_rows)
        acc_ref[rows, :] += term

    @pl.when(step == pl.num_programs(0) - 1)
    def _():
        out_ref[...] = acc_ref[...].astype(out_ref.dtype)


def _aggregate(acc, adj, msgs, inv, tb, k, final, group=16):
    steps, block_rows, n_dim = msgs.shape
    rows = acc.shape[0]
    out_dtype = jnp.bfloat16 if final else jnp.float32
    grid_spec = pltpu.PrefetchScalarGridSpec(
        num_scalar_prefetch=1,
        grid=(steps // group,),
        in_specs=[
            pl.BlockSpec((group, None, block_rows, block_rows), lambda i, t: (i, k, 0, 0)),
            pl.BlockSpec((group, block_rows, n_dim), lambda i, t: (i, 0, 0)),
            pl.BlockSpec((group, block_rows, 1), lambda i, t: (i, 0, 0)),
            pl.BlockSpec((rows, n_dim), lambda i, t: (0, 0), pipeline_mode=pl.Buffered(1)),
        ],
        out_specs=pl.BlockSpec((rows, n_dim), lambda i, t: (0, 0)),
    )
    cost = pl.CostEstimate(
        flops=2 * steps * block_rows * block_rows * n_dim,
        bytes_accessed=steps * block_rows * (block_rows * 2 + n_dim * 2 + 4)
        + rows * n_dim * (4 + jnp.dtype(out_dtype).itemsize),
        transcendentals=0,
    )
    return pl.pallas_call(
        functools.partial(_agg_kernel, group, final),
        grid_spec=grid_spec,
        out_shape=jax.ShapeDtypeStruct(acc.shape, out_dtype),
        compiler_params=pltpu.CompilerParams(
            dimension_semantics=("arbitrary",), vmem_limit_bytes=56 * 1024 * 1024
        ),
        cost_estimate=cost,
    )(tb, adj, msgs, inv, acc)


def _with_partner(x):
    return x, lax.ppermute(x, "col", [(0, 1), (1, 0)])


def on_device(
    features,
    block_type,
    rel_weight,
    self_weight,
    source_relation,
    source_block,
    target_relation,
    target_block,
    live,
    tiles,
):
    blk_count = block_type.shape[0]
    rows_total = features.shape[0]
    block_rows = rows_total // blk_count
    relations = rel_weight.shape[0]
    partitions = live.shape[1]
    capacity = live.shape[2]
    slots = partitions * capacity

    full_rows = _with_partner(features)

    tiles4 = tiles.reshape(partitions, capacity, block_rows, block_rows)
    live2 = live.reshape(partitions, capacity)
    row_sums = (jnp.sum(tiles4, axis=3) * live2[:, :, None]).astype(jnp.float32)
    keys = target_relation.reshape(slots) * blk_count + target_block.reshape(slots)
    table = (keys[:, None] == jnp.arange(relations * blk_count)[None, :]).astype(jnp.float32)
    degree = jnp.dot(
        table.T, row_sums.reshape(slots, block_rows), precision=lax.Precision.HIGHEST
    )
    inverse = 1.0 / jnp.maximum(degree, 1.0)
    scale = jnp.dot(table, inverse, precision=lax.Precision.HIGHEST)
    scale = scale.reshape(partitions, capacity, block_rows, 1)

    src_blocks = source_block.reshape(partitions, capacity)
    src_rels = source_relation.reshape(partitions, capacity)
    dst_blocks = target_block.reshape(partitions, capacity)

    raw = _pick_blocks(features, src_blocks[:, 0], block_rows)
    arrived = [lax.all_to_all(raw, "dom", split_axis=0, concat_axis=0, tiled=True)]
    for k in range(1, capacity):
        msgs = _block_matmul(
            full_rows, rel_weight, src_blocks[:, k], src_rels[:, k], block_rows, jnp.bfloat16
        )
        arrived[0], msgs = lax.optimization_barrier((arrived[0], msgs))
        arrived.append(lax.all_to_all(msgs, "dom", split_axis=0, concat_axis=0, tiled=True))

    selfs = _block_matmul(
        full_rows,
        self_weight,
        jnp.arange(blk_count, dtype=jnp.int32),
        block_type,
        block_rows,
        jnp.float32,
    )
    acc = selfs.reshape(rows_total, selfs.shape[2])
    mine, other = _with_partner(arrived[0])
    arrived[0] = _block_matmul(
        (
            mine.reshape(partitions * block_rows, mine.shape[2]),
            other.reshape(partitions * block_rows, other.shape[2]),
        ),
        rel_weight,
        jnp.arange(partitions, dtype=jnp.int32),
        target_relation.reshape(partitions, capacity)[:, 0],
        block_rows,
        jnp.bfloat16,
    )
    adjacency = (tiles4 * live2[:, :, None, None]).astype(jnp.bfloat16)
    for k in range(capacity):
        acc = _aggregate(
            acc,
            adjacency,
            arrived[k],
            scale[:, k],
            dst_blocks[:, k],
            k,
            final=k == capacity - 1,
        )
    return acc


def solution(mesh):
    in_specs = (
        P("dom", "col"),
        P("dom"),
        P(None, None, "col"),
        P(None, None, "col"),
        P("dom", None, None),
        P("dom", None, None),
        P("dom", None, None),
        P("dom", None, None),
        P("dom", None, None),
        P("dom", None, None, None, None),
    )
    out_specs = P("dom", "col")
    return jax.shard_map(
        on_device, mesh=mesh, in_specs=in_specs, out_specs=out_specs, check_vma=False
    )
```

```python
import functools

import jax
import jax.numpy as jnp
from jax import lax
from jax.experimental import pallas as pl
from jax.experimental.pallas import tpu as pltpu
from jax.sharding import PartitionSpec as P


def _bmm_kernel(group, src_ref, widx_ref, col_ref, mine_ref, other_ref, w_ref, o_ref):
    step = pl.program_id(0)
    block_rows = o_ref.shape[1]
    first = col_ref[0] == 0
    for j in range(group):
        slot = step * group + j
        rows = pl.ds(pl.multiple_of(src_ref[slot] * block_rows, block_rows), block_rows)
        mine = mine_ref[rows, :]
        other = other_ref[rows, :]
        x = jnp.concatenate(
            [jnp.where(first, mine, other), jnp.where(first, other, mine)], axis=1
        )
        o_ref[j] = jnp.dot(
            x, w_ref[widx_ref[slot]], preferred_element_type=jnp.float32
        ).astype(o_ref.dtype)


def _block_matmul(halves, w, src, widx, block_rows, out_dtype, group=8):
    mine, other = halves
    k_dim = 2 * mine.shape[1]
    n_dim = w.shape[2]
    steps = src.shape[0]
    col = lax.axis_index("col").astype(jnp.int32).reshape(1)
    grid_spec = pltpu.PrefetchScalarGridSpec(
        num_scalar_prefetch=3,
        grid=(steps // group,),
        in_specs=[
            pl.BlockSpec(mine.shape, lambda i, r, g, c: (0, 0), pipeline_mode=pl.Buffered(1)),
            pl.BlockSpec(other.shape, lambda i, r, g, c: (0, 0), pipeline_mode=pl.Buffered(1)),
            pl.BlockSpec(w.shape, lambda i, r, g, c: (0, 0, 0), pipeline_mode=pl.Buffered(1)),
        ],
        out_specs=pl.BlockSpec((group, block_rows, n_dim), lambda i, r, g, c: (i, 0, 0)),
    )
    out_bytes = jnp.dtype(out_dtype).itemsize
    cost = pl.CostEstimate(
        flops=2 * steps * block_rows * k_dim * n_dim,
        bytes_accessed=mine.size * 4 + w.size * 2 + steps * block_rows * n_dim * out_bytes,
        transcendentals=0,
    )
    return pl.pallas_call(
        functools.partial(_bmm_kernel, group),
        grid_spec=grid_spec,
        out_shape=jax.ShapeDtypeStruct((steps, block_rows, n_dim), out_dtype),
        compiler_params=pltpu.CompilerParams(
            dimension_semantics=("arbitrary",), vmem_limit_bytes=56 * 1024 * 1024
        ),
        cost_estimate=cost,
    )(src, widx, col, mine, other, w)


def _pick_kernel(group, src_ref, x_ref, o_ref):
    step = pl.program_id(0)
    block_rows = o_ref.shape[1]
    for j in range(group):
        rows = pl.ds(pl.multiple_of(src_ref[step * group + j] * block_rows, block_rows), block_rows)
        o_ref[j] = x_ref[rows, :]


def _pick_blocks(x, src, block_rows, group=8):
    steps = src.shape[0]
    grid_spec = pltpu.PrefetchScalarGridSpec(
        num_scalar_prefetch=1,
        grid=(steps // group,),
        in_specs=[pl.BlockSpec(x.shape, lambda i, r: (0, 0), pipeline_mode=pl.Buffered(1))],
        out_specs=pl.BlockSpec((group, block_rows, x.shape[1]), lambda i, r: (i, 0, 0)),
    )
    return pl.pallas_call(
        functools.partial(_pick_kernel, group),
        grid_spec=grid_spec,
        out_shape=jax.ShapeDtypeStruct((steps, block_rows, x.shape[1]), x.dtype),
        compiler_params=pltpu.CompilerParams(dimension_semantics=("arbitrary",)),
        cost_estimate=pl.CostEstimate(
            flops=0, bytes_accessed=x.size * 2 + steps * block_rows * x.shape[1] * 2,
            transcendentals=0,
        ),
    )(src, x)


def _agg_kernel(group, final, tb_ref, adj_ref, msg_ref, inv_ref, acc_ref, out_ref):
    step = pl.program_id(0)
    block_rows = msg_ref.shape[1]
    for j in range(group):
        slot = step * group + j
        scale = jnp.transpose(jnp.broadcast_to(inv_ref[j], (block_rows, block_rows)))
        term = jnp.dot(adj_ref[j], msg_ref[j], preferred_element_type=jnp.float32)
        lanes = scale.shape[1]
        term = jnp.concatenate(
            [term[:, c : c + lanes] * scale for c in range(0, term.shape[1], lanes)], axis=1
        )
        rows = pl.ds(pl.multiple_of(tb_ref[slot] * block_rows, block_rows), block_rows)
        acc_ref[rows, :] += term

    @pl.when(step == pl.num_programs(0) - 1)
    def _():
        out_ref[...] = acc_ref[...].astype(out_ref.dtype)


def _aggregate(acc, adj, msgs, inv, tb, k, final, group=16):
    steps, block_rows, n_dim = msgs.shape
    rows = acc.shape[0]
    out_dtype = jnp.bfloat16 if final else jnp.float32
    grid_spec = pltpu.PrefetchScalarGridSpec(
        num_scalar_prefetch=1,
        grid=(steps // group,),
        in_specs=[
            pl.BlockSpec((group, None, block_rows, block_rows), lambda i, t: (i, k, 0, 0)),
            pl.BlockSpec((group, block_rows, n_dim), lambda i, t: (i, 0, 0)),
            pl.BlockSpec((group, 1, block_rows), lambda i, t: (i, 0, 0)),
            pl.BlockSpec((rows, n_dim), lambda i, t: (0, 0), pipeline_mode=pl.Buffered(1)),
        ],
        out_specs=pl.BlockSpec((rows, n_dim), lambda i, t: (0, 0)),
    )
    cost = pl.CostEstimate(
        flops=2 * steps * block_rows * block_rows * n_dim,
        bytes_accessed=steps * block_rows * (block_rows * 2 + n_dim * 2 + 4)
        + rows * n_dim * (4 + jnp.dtype(out_dtype).itemsize),
        transcendentals=0,
    )
    return pl.pallas_call(
        functools.partial(_agg_kernel, group, final),
        grid_spec=grid_spec,
        out_shape=jax.ShapeDtypeStruct(acc.shape, out_dtype),
        compiler_params=pltpu.CompilerParams(
            dimension_semantics=("arbitrary",), vmem_limit_bytes=56 * 1024 * 1024
        ),
        cost_estimate=cost,
    )(tb, adj, msgs, inv, acc)


def _with_partner(x):
    return x, lax.ppermute(x, "col", [(0, 1), (1, 0)])


def on_device(
    features,
    block_type,
    rel_weight,
    self_weight,
    source_relation,
    source_block,
    target_relation,
    target_block,
    live,
    tiles,
):
    blk_count = block_type.shape[0]
    rows_total = features.shape[0]
    block_rows = rows_total // blk_count
    relations = rel_weight.shape[0]
    partitions = live.shape[1]
    capacity = live.shape[2]
    slots = partitions * capacity

    full_rows = _with_partner(features)

    tiles4 = tiles.reshape(partitions, capacity, block_rows, block_rows)
    live2 = live.reshape(partitions, capacity)
    row_sums = (jnp.sum(tiles4, axis=3) * live2[:, :, None]).astype(jnp.float32)
    keys = target_relation.reshape(slots) * blk_count + target_block.reshape(slots)
    table = (keys[:, None] == jnp.arange(relations * blk_count)[None, :]).astype(jnp.float32)
    degree = jnp.dot(
        table.T, row_sums.reshape(slots, block_rows), precision=lax.Precision.HIGHEST
    )
    inverse = 1.0 / jnp.maximum(degree, 1.0)
    scale = jnp.dot(table, inverse, precision=lax.Precision.HIGHEST)
    scale = scale.reshape(partitions, capacity, 1, block_rows)

    src_blocks = source_block.reshape(partitions, capacity)
    src_rels = source_relation.reshape(partitions, capacity)
    dst_blocks = target_block.reshape(partitions, capacity)

    raw = _pick_blocks(features, src_blocks[:, 0], block_rows)
    arrived = [lax.all_to_all(raw, "dom", split_axis=0, concat_axis=0, tiled=True)]
    for k in range(1, capacity):
        msgs = _block_matmul(
            full_rows, rel_weight, src_blocks[:, k], src_rels[:, k], block_rows, jnp.bfloat16
        )
        arrived[0], msgs = lax.optimization_barrier((arrived[0], msgs))
        arrived.append(lax.all_to_all(msgs, "dom", split_axis=0, concat_axis=0, tiled=True))

    selfs = _block_matmul(
        full_rows,
        self_weight,
        jnp.arange(blk_count, dtype=jnp.int32),
        block_type,
        block_rows,
        jnp.float32,
    )
    acc = selfs.reshape(rows_total, selfs.shape[2])
    mine, other = _with_partner(arrived[0])
    arrived[0] = _block_matmul(
        (
            mine.reshape(partitions * block_rows, mine.shape[2]),
            other.reshape(partitions * block_rows, other.shape[2]),
        ),
        rel_weight,
        jnp.arange(partitions, dtype=jnp.int32),
        target_relation.reshape(partitions, capacity)[:, 0],
        block_rows,
        jnp.bfloat16,
    )
    adjacency = (tiles4 * live2[:, :, None, None]).astype(jnp.bfloat16)
    for k in range(capacity):
        acc = _aggregate(
            acc,
            adjacency,
            arrived[k],
            scale[:, k],
            dst_blocks[:, k],
            k,
            final=k == capacity - 1,
        )
    return acc


def solution(mesh):
    in_specs = (
        P("dom", "col"),
        P("dom"),
        P(None, None, "col"),
        P(None, None, "col"),
        P("dom", None, None),
        P("dom", None, None),
        P("dom", None, None),
        P("dom", None, None),
        P("dom", None, None),
        P("dom", None, None, None, None),
    )
    out_specs = P("dom", "col")
    return jax.shard_map(
        on_device, mesh=mesh, in_specs=in_specs, out_specs=out_specs, check_vma=False
    )
```

```python
import functools

import jax
import jax.numpy as jnp
from jax import lax
from jax.experimental import pallas as pl
from jax.experimental.pallas import tpu as pltpu
from jax.sharding import PartitionSpec as P


def _bmm_kernel(group, src_ref, widx_ref, col_ref, mine_ref, other_ref, w_ref, o_ref):
    step = pl.program_id(0)
    block_rows = o_ref.shape[1]
    first = col_ref[0] == 0
    for j in range(group):
        slot = step * group + j
        rows = pl.ds(pl.multiple_of(src_ref[slot] * block_rows, block_rows), block_rows)
        mine = mine_ref[rows, :]
        other = other_ref[rows, :]
        x = jnp.concatenate(
            [jnp.where(first, mine, other), jnp.where(first, other, mine)], axis=1
        )
        o_ref[j] = jnp.dot(
            x, w_ref[widx_ref[slot]], preferred_element_type=jnp.float32
        ).astype(o_ref.dtype)


def _block_matmul(halves, w, src, widx, block_rows, out_dtype, group=8):
    mine, other = halves
    k_dim = 2 * mine.shape[1]
    n_dim = w.shape[2]
    steps = src.shape[0]
    col = lax.axis_index("col").astype(jnp.int32).reshape(1)
    grid_spec = pltpu.PrefetchScalarGridSpec(
        num_scalar_prefetch=3,
        grid=(steps // group,),
        in_specs=[
            pl.BlockSpec(mine.shape, lambda i, r, g, c: (0, 0), pipeline_mode=pl.Buffered(1)),
            pl.BlockSpec(other.shape, lambda i, r, g, c: (0, 0), pipeline_mode=pl.Buffered(1)),
            pl.BlockSpec(w.shape, lambda i, r, g, c: (0, 0, 0), pipeline_mode=pl.Buffered(1)),
        ],
        out_specs=pl.BlockSpec((group, block_rows, n_dim), lambda i, r, g, c: (i, 0, 0)),
    )
    out_bytes = jnp.dtype(out_dtype).itemsize
    cost = pl.CostEstimate(
        flops=2 * steps * block_rows * k_dim * n_dim,
        bytes_accessed=mine.size * 4 + w.size * 2 + steps * block_rows * n_dim * out_bytes,
        transcendentals=0,
    )
    return pl.pallas_call(
        functools.partial(_bmm_kernel, group),
        grid_spec=grid_spec,
        out_shape=jax.ShapeDtypeStruct((steps, block_rows, n_dim), out_dtype),
        compiler_params=pltpu.CompilerParams(
            dimension_semantics=("arbitrary",), vmem_limit_bytes=56 * 1024 * 1024
        ),
        cost_estimate=cost,
    )(src, widx, col, mine, other, w)


def _pick_kernel(group, src_ref, x_ref, o_ref):
    step = pl.program_id(0)
    block_rows = o_ref.shape[1]
    for j in range(group):
        rows = pl.ds(pl.multiple_of(src_ref[step * group + j] * block_rows, block_rows), block_rows)
        o_ref[j] = x_ref[rows, :]


def _pick_blocks(x, src, block_rows, group=16):
    steps = src.shape[0]
    grid_spec = pltpu.PrefetchScalarGridSpec(
        num_scalar_prefetch=1,
        grid=(steps // group,),
        in_specs=[pl.BlockSpec(x.shape, lambda i, r: (0, 0), pipeline_mode=pl.Buffered(1))],
        out_specs=pl.BlockSpec((group, block_rows, x.shape[1]), lambda i, r: (i, 0, 0)),
    )
    return pl.pallas_call(
        functools.partial(_pick_kernel, group),
        grid_spec=grid_spec,
        out_shape=jax.ShapeDtypeStruct((steps, block_rows, x.shape[1]), x.dtype),
        compiler_params=pltpu.CompilerParams(dimension_semantics=("arbitrary",)),
        cost_estimate=pl.CostEstimate(
            flops=0, bytes_accessed=x.size * 2 + steps * block_rows * x.shape[1] * 2,
            transcendentals=0,
        ),
    )(src, x)


def _agg_kernel(group, final, tb_ref, adj_ref, msg_ref, inv_ref, acc_ref, out_ref):
    step = pl.program_id(0)
    block_rows = msg_ref.shape[1]
    for j in range(group):
        slot = step * group + j
        scale = jnp.transpose(jnp.broadcast_to(inv_ref[j], (block_rows, block_rows)))
        term = jnp.dot(adj_ref[j], msg_ref[j], preferred_element_type=jnp.float32)
        lanes = scale.shape[1]
        term = jnp.concatenate(
            [term[:, c : c + lanes] * scale for c in range(0, term.shape[1], lanes)], axis=1
        )
        rows = pl.ds(pl.multiple_of(tb_ref[slot] * block_rows, block_rows), block_rows)
        acc_ref[rows, :] += term

    @pl.when(step == pl.num_programs(0) - 1)
    def _():
        out_ref[...] = acc_ref[...].astype(out_ref.dtype)


def _aggregate(acc, adj, msgs, inv, tb, k, final, group=32):
    steps, block_rows, n_dim = msgs.shape
    rows = acc.shape[0]
    out_dtype = jnp.bfloat16 if final else jnp.float32
    grid_spec = pltpu.PrefetchScalarGridSpec(
        num_scalar_prefetch=1,
        grid=(steps // group,),
        in_specs=[
            pl.BlockSpec((group, None, block_rows, block_rows), lambda i, t: (i, k, 0, 0)),
            pl.BlockSpec((group, block_rows, n_dim), lambda i, t: (i, 0, 0)),
            pl.BlockSpec((group, 1, block_rows), lambda i, t: (i, 0, 0)),
            pl.BlockSpec((rows, n_dim), lambda i, t: (0, 0), pipeline_mode=pl.Buffered(1)),
        ],
        out_specs=pl.BlockSpec((rows, n_dim), lambda i, t: (0, 0)),
    )
    cost = pl.CostEstimate(
        flops=2 * steps * block_rows * block_rows * n_dim,
        bytes_accessed=steps * block_rows * (block_rows * 2 + n_dim * 2 + 4)
        + rows * n_dim * (4 + jnp.dtype(out_dtype).itemsize),
        transcendentals=0,
    )
    return pl.pallas_call(
        functools.partial(_agg_kernel, group, final),
        grid_spec=grid_spec,
        out_shape=jax.ShapeDtypeStruct(acc.shape, out_dtype),
        compiler_params=pltpu.CompilerParams(
            dimension_semantics=("arbitrary",), vmem_limit_bytes=56 * 1024 * 1024
        ),
        cost_estimate=cost,
    )(tb, adj, msgs, inv, acc)


def _with_partner(x):
    return x, lax.ppermute(x, "col", [(0, 1), (1, 0)])


def on_device(
    features,
    block_type,
    rel_weight,
    self_weight,
    source_relation,
    source_block,
    target_relation,
    target_block,
    live,
    tiles,
):
    blk_count = block_type.shape[0]
    rows_total = features.shape[0]
    block_rows = rows_total // blk_count
    relations = rel_weight.shape[0]
    partitions = live.shape[1]
    capacity = live.shape[2]
    slots = partitions * capacity

    full_rows = _with_partner(features)

    tiles4 = tiles.reshape(partitions, capacity, block_rows, block_rows)
    live2 = live.reshape(partitions, capacity)
    row_sums = (jnp.sum(tiles4, axis=3) * live2[:, :, None]).astype(jnp.float32)
    keys = target_relation.reshape(slots) * blk_count + target_block.reshape(slots)
    table = (keys[:, None] == jnp.arange(relations * blk_count)[None, :]).astype(jnp.float32)
    degree = jnp.dot(
        table.T, row_sums.reshape(slots, block_rows), precision=lax.Precision.HIGHEST
    )
    inverse = 1.0 / jnp.maximum(degree, 1.0)
    scale = jnp.dot(table, inverse, precision=lax.Precision.HIGHEST)
    scale = scale.reshape(partitions, capacity, 1, block_rows)

    src_blocks = source_block.reshape(partitions, capacity)
    src_rels = source_relation.reshape(partitions, capacity)
    dst_blocks = target_block.reshape(partitions, capacity)

    raw = _pick_blocks(features, src_blocks[:, 0], block_rows)
    arrived = [lax.all_to_all(raw, "dom", split_axis=0, concat_axis=0, tiled=True)]
    for k in range(1, capacity):
        msgs = _block_matmul(
            full_rows, rel_weight, src_blocks[:, k], src_rels[:, k], block_rows, jnp.bfloat16
        )
        arrived[0], msgs = lax.optimization_barrier((arrived[0], msgs))
        arrived.append(lax.all_to_all(msgs, "dom", split_axis=0, concat_axis=0, tiled=True))

    selfs = _block_matmul(
        full_rows,
        self_weight,
        jnp.arange(blk_count, dtype=jnp.int32),
        block_type,
        block_rows,
        jnp.float32,
    )
    acc = selfs.reshape(rows_total, selfs.shape[2])
    mine, other = _with_partner(arrived[0])
    arrived[0] = _block_matmul(
        (
            mine.reshape(partitions * block_rows, mine.shape[2]),
            other.reshape(partitions * block_rows, other.shape[2]),
        ),
        rel_weight,
        jnp.arange(partitions, dtype=jnp.int32),
        target_relation.reshape(partitions, capacity)[:, 0],
        block_rows,
        jnp.bfloat16,
    )
    adjacency = (tiles4 * live2[:, :, None, None]).astype(jnp.bfloat16)
    for k in range(capacity):
        acc = _aggregate(
            acc,
            adjacency,
            arrived[k],
            scale[:, k],
            dst_blocks[:, k],
            k,
            final=k == capacity - 1,
        )
    return acc


def solution(mesh):
    in_specs = (
        P("dom", "col"),
        P("dom"),
        P(None, None, "col"),
        P(None, None, "col"),
        P("dom", None, None),
        P("dom", None, None),
        P("dom", None, None),
        P("dom", None, None),
        P("dom", None, None),
        P("dom", None, None, None, None),
    )
    out_specs = P("dom", "col")
    return jax.shard_map(
        on_device, mesh=mesh, in_specs=in_specs, out_specs=out_specs, check_vma=False
    )
```

```python
import functools

import jax
import jax.numpy as jnp
from jax import lax
from jax.experimental import pallas as pl
from jax.experimental.pallas import tpu as pltpu
from jax.sharding import PartitionSpec as P


def _bmm_kernel(group, src_ref, widx_ref, col_ref, mine_ref, other_ref, w_ref, o_ref):
    step = pl.program_id(0)
    block_rows = o_ref.shape[1]
    first = col_ref[0] == 0
    for j in range(group):
        slot = step * group + j
        rows = pl.ds(pl.multiple_of(src_ref[slot] * block_rows, block_rows), block_rows)
        mine = mine_ref[rows, :]
        other = other_ref[rows, :]
        x = jnp.concatenate(
            [jnp.where(first, mine, other), jnp.where(first, other, mine)], axis=1
        )
        o_ref[j] = jnp.dot(
            x, w_ref[widx_ref[slot]], preferred_element_type=jnp.float32
        ).astype(o_ref.dtype)


def _block_matmul(halves, w, src, widx, block_rows, out_dtype, group=8):
    mine, other = halves
    k_dim = 2 * mine.shape[1]
    n_dim = w.shape[2]
    steps = src.shape[0]
    col = lax.axis_index("col").astype(jnp.int32).reshape(1)
    grid_spec = pltpu.PrefetchScalarGridSpec(
        num_scalar_prefetch=3,
        grid=(steps // group,),
        in_specs=[
            pl.BlockSpec(mine.shape, lambda i, r, g, c: (0, 0), pipeline_mode=pl.Buffered(1)),
            pl.BlockSpec(other.shape, lambda i, r, g, c: (0, 0), pipeline_mode=pl.Buffered(1)),
            pl.BlockSpec(w.shape, lambda i, r, g, c: (0, 0, 0), pipeline_mode=pl.Buffered(1)),
        ],
        out_specs=pl.BlockSpec((group, block_rows, n_dim), lambda i, r, g, c: (i, 0, 0)),
    )
    out_bytes = jnp.dtype(out_dtype).itemsize
    cost = pl.CostEstimate(
        flops=2 * steps * block_rows * k_dim * n_dim,
        bytes_accessed=mine.size * 4 + w.size * 2 + steps * block_rows * n_dim * out_bytes,
        transcendentals=0,
    )
    return pl.pallas_call(
        functools.partial(_bmm_kernel, group),
        grid_spec=grid_spec,
        out_shape=jax.ShapeDtypeStruct((steps, block_rows, n_dim), out_dtype),
        compiler_params=pltpu.CompilerParams(
            dimension_semantics=("arbitrary",), vmem_limit_bytes=56 * 1024 * 1024
        ),
        cost_estimate=cost,
    )(src, widx, col, mine, other, w)


def _pick_kernel(group, src_ref, x_ref, o_ref):
    step = pl.program_id(0)
    block_rows = o_ref.shape[1]
    for j in range(group):
        rows = pl.ds(pl.multiple_of(src_ref[step * group + j] * block_rows, block_rows), block_rows)
        o_ref[j] = x_ref[rows, :]


def _pick_blocks(x, src, steps, block_rows, group=16):
    grid_spec = pltpu.PrefetchScalarGridSpec(
        num_scalar_prefetch=1,
        grid=(steps // group,),
        in_specs=[pl.BlockSpec(x.shape, lambda i, r: (0, 0), pipeline_mode=pl.Buffered(1))],
        out_specs=pl.BlockSpec((group, block_rows, x.shape[1]), lambda i, r: (i, 0, 0)),
    )
    return pl.pallas_call(
        functools.partial(_pick_kernel, group),
        grid_spec=grid_spec,
        out_shape=jax.ShapeDtypeStruct((steps, block_rows, x.shape[1]), x.dtype),
        compiler_params=pltpu.CompilerParams(dimension_semantics=("arbitrary",)),
        cost_estimate=pl.CostEstimate(
            flops=0, bytes_accessed=x.size * 2 + steps * block_rows * x.shape[1] * 2,
            transcendentals=0,
        ),
    )(src, x)


def _agg_kernel(group, final, tb_ref, adj_ref, msg_ref, inv_ref, acc_ref, out_ref):
    step = pl.program_id(0)
    block_rows = msg_ref.shape[1]
    for j in range(group):
        slot = step * group + j
        scale = jnp.transpose(jnp.broadcast_to(inv_ref[j], (block_rows, block_rows)))
        term = jnp.dot(adj_ref[j], msg_ref[j], preferred_element_type=jnp.float32)
        lanes = scale.shape[1]
        term = jnp.concatenate(
            [term[:, c : c + lanes] * scale for c in range(0, term.shape[1], lanes)], axis=1
        )
        rows = pl.ds(pl.multiple_of(tb_ref[slot] * block_rows, block_rows), block_rows)
        acc_ref[rows, :] += term

    @pl.when(step == pl.num_programs(0) - 1)
    def _():
        out_ref[...] = acc_ref[...].astype(out_ref.dtype)


def _aggregate(acc, adj, msgs, inv, tb, k, final, group=32):
    steps, block_rows, n_dim = msgs.shape
    rows = acc.shape[0]
    out_dtype = jnp.bfloat16 if final else jnp.float32
    grid_spec = pltpu.PrefetchScalarGridSpec(
        num_scalar_prefetch=1,
        grid=(steps // group,),
        in_specs=[
            pl.BlockSpec((group, None, block_rows, block_rows), lambda i, t: (i, k, 0, 0)),
            pl.BlockSpec((group, block_rows, n_dim), lambda i, t: (i, 0, 0)),
            pl.BlockSpec((group, 1, block_rows), lambda i, t: (i, 0, 0)),
            pl.BlockSpec((rows, n_dim), lambda i, t: (0, 0), pipeline_mode=pl.Buffered(1)),
        ],
        out_specs=pl.BlockSpec((rows, n_dim), lambda i, t: (0, 0)),
    )
    cost = pl.CostEstimate(
        flops=2 * steps * block_rows * block_rows * n_dim,
        bytes_accessed=steps * block_rows * (block_rows * 2 + n_dim * 2 + 4)
        + rows * n_dim * (4 + jnp.dtype(out_dtype).itemsize),
        transcendentals=0,
    )
    return pl.pallas_call(
        functools.partial(_agg_kernel, group, final),
        grid_spec=grid_spec,
        out_shape=jax.ShapeDtypeStruct(acc.shape, out_dtype),
        compiler_params=pltpu.CompilerParams(
            dimension_semantics=("arbitrary",), vmem_limit_bytes=56 * 1024 * 1024
        ),
        cost_estimate=cost,
    )(tb, adj, msgs, inv, acc)


def _with_partner(x):
    return x, lax.ppermute(x, "col", [(0, 1), (1, 0)])


def on_device(
    features,
    block_type,
    rel_weight,
    self_weight,
    source_relation,
    source_block,
    target_relation,
    target_block,
    live,
    tiles,
):
    blk_count = block_type.shape[0]
    rows_total = features.shape[0]
    block_rows = rows_total // blk_count
    relations = rel_weight.shape[0]
    partitions = live.shape[1]
    capacity = live.shape[2]
    slots = partitions * capacity

    full_rows = _with_partner(features)

    tiles4 = tiles.reshape(partitions, capacity, block_rows, block_rows)
    live2 = live.reshape(partitions, capacity)
    row_sums = (jnp.sum(tiles4, axis=3) * live2[:, :, None]).astype(jnp.float32)
    keys = target_relation.reshape(slots) * blk_count + target_block.reshape(slots)
    table = (keys[:, None] == jnp.arange(relations * blk_count)[None, :]).astype(jnp.float32)
    degree = jnp.dot(
        table.T, row_sums.reshape(slots, block_rows), precision=lax.Precision.HIGHEST
    )
    inverse = 1.0 / jnp.maximum(degree, 1.0)
    scale = jnp.dot(table, inverse, precision=lax.Precision.HIGHEST)
    scale = scale.reshape(partitions, capacity, 1, block_rows)

    src_blocks = source_block.reshape(partitions, capacity)
    src_rels = source_relation.reshape(partitions, capacity)
    dst_blocks = target_block.reshape(partitions, capacity)

    raw = _pick_blocks(features, jnp.transpose(src_blocks).reshape(slots), partitions, block_rows)
    arrived = [lax.all_to_all(raw, "dom", split_axis=0, concat_axis=0, tiled=True)]
    for k in range(1, capacity):
        msgs = _block_matmul(
            full_rows, rel_weight, src_blocks[:, k], src_rels[:, k], block_rows, jnp.bfloat16
        )
        arrived[0], msgs = lax.optimization_barrier((arrived[0], msgs))
        arrived.append(lax.all_to_all(msgs, "dom", split_axis=0, concat_axis=0, tiled=True))

    selfs = _block_matmul(
        full_rows,
        self_weight,
        jnp.arange(blk_count, dtype=jnp.int32),
        block_type,
        block_rows,
        jnp.float32,
    )
    acc = selfs.reshape(rows_total, selfs.shape[2])
    mine, other = _with_partner(arrived[0])
    arrived[0] = _block_matmul(
        (
            mine.reshape(partitions * block_rows, mine.shape[2]),
            other.reshape(partitions * block_rows, other.shape[2]),
        ),
        rel_weight,
        jnp.arange(partitions, dtype=jnp.int32),
        target_relation.reshape(partitions, capacity)[:, 0],
        block_rows,
        jnp.bfloat16,
    )
    adjacency = (tiles4 * live2[:, :, None, None]).astype(jnp.bfloat16)
    for k in range(capacity):
        acc = _aggregate(
            acc,
            adjacency,
            arrived[k],
            scale[:, k],
            dst_blocks[:, k],
            k,
            final=k == capacity - 1,
        )
    return acc


def solution(mesh):
    in_specs = (
        P("dom", "col"),
        P("dom"),
        P(None, None, "col"),
        P(None, None, "col"),
        P("dom", None, None),
        P("dom", None, None),
        P("dom", None, None),
        P("dom", None, None),
        P("dom", None, None),
        P("dom", None, None, None, None),
    )
    out_specs = P("dom", "col")
    return jax.shard_map(
        on_device, mesh=mesh, in_specs=in_specs, out_specs=out_specs, check_vma=False
    )
```
